32 devices in a mesh: gx: 8 (over z, x), gy: 4 (over y, core).
Axes of the slice: x: 2, y: 2, z: 4, core: 2. Of those that a mesh axis runs over, the one named last changes fastest.
Arguments:
- fields: bfloat16 [4, 64, 128, 256], P(None, 'gx', 'gy'), may hold values from -6 to 6
- rows_live: int32 [8], replicated, may hold values from 4 to 8, as said below
- cols_live: int32 [4], replicated, may hold values from 16 to 32, as said below
- weight: bfloat16 [32, 108], replicated, may hold values from -0.625 to 0.625
- bias: float32 [32], replicated, may hold values from -3 to 3
- grad_out: bfloat16 [32, 32, 64, 128], P('gy', 'gx'), may hold values from -0.0625 to 0.0625
Outputs:
- stem: bfloat16 [32, 32, 64, 128], P('gy', 'gx')
- weight_grad: float32 [32, 108], P('gy')
- bias_grad: float32 [32], P('gy')
The draws below stay inside these ranges and needn't reach their ends.
Inputs may be any that keep to these rules, and one draw needn't show every extreme that they name: `rows_live`: every entry is even, and some entry equals 8. `cols_live`: every entry is even, and some entry equals 32.
All inputs are finite; a program needn't handle non-finite values.
Results may differ from the reference program's by a relative error of at most 0.0054.
Values may be sent and summed in bfloat16 or wider, within the bound.
No kernel may reach another device: no remote copies, remote signals or barrier semaphores. Data moves between devices by JAX's collectives and lax.ppermute only.
A program may use at most 64 MiB of HBM per device.

```python
import jax
import jax.numpy as jnp
from jax import lax

CIN = 4
COUT = 32
CAPX = 8
CAPY = 32
Z = 256
X = 64
Y = 128
X2 = 32
Y2 = 64
Z2 = 128
N_GX = 8
N_GY = 4


def live_counts(key, tiles, capacity):
    key_counts, key_full = jax.random.split(key)
    counts = 2 * jax.random.randint(key_counts, (tiles,), capacity // 4, capacity // 2 + 1)
    full_at = jax.random.randint(key_full, (), 0, tiles)
    return jnp.where(jnp.arange(tiles) == full_at, capacity, counts).astype(jnp.int32)


def draw_rows_live(key, part):
    return live_counts(jax.random.fold_in(key, 3), N_GX, CAPX)


def draw_cols_live(key, part):
    return live_counts(jax.random.fold_in(key, 7), N_GY, CAPY)


def raised(drawn, key, source, target, blocks, factor):
    owner, partner = [(jnp.arange(drawn.shape[position]) // (drawn.shape[position] // blocks)).reshape([-1 if axis == position else 1 for axis in range(drawn.ndim)]) for position in (source, target)]
    chosen = jax.random.permutation(key, blocks)[partner]
    strong = (owner == chosen) | (owner == (partner + blocks // 2) % blocks)
    return jnp.where(strong, factor * drawn, drawn)


def steps_of(own_key, extent, cuts, least, high):
    level = 1.0
    for axis_at, shards_of in cuts:
        heights = jax.random.uniform(jax.random.fold_in(jax.random.fold_in(own_key, 6), axis_at), (shards_of,), jnp.float32, least / len(cuts), high / len(cuts))
        level = level * jnp.repeat(jnp.exp(heights), extent[axis_at] // shards_of).reshape((-1,) + (1,) * (len(extent) - 1 - axis_at))
    return level


def normal_values(key, dims, deviation, reach, cuts=(), held_as=jnp.bfloat16):
    result = deviation * jax.random.normal(key, dims, jnp.float32)
    if cuts:
        result = result * steps_of(key, dims, cuts, -0.22, 0.18)
    return jnp.clip(result, -reach, reach).astype(held_as)


def bell_draw_with(key, extent, deviation, most, cuts, heavy, held_as=jnp.bfloat16):
    entries = deviation * jax.random.normal(key, extent, jnp.float32)
    if cuts:
        entries = entries * steps_of(key, extent, cuts, -0.22, 0.18)
    return jnp.clip(raised(entries, jax.random.fold_in(key, 3), *heavy), -most, most).astype(held_as)


def setup_inputs(seed: int = 0) -> dict:
    key_of = jax.random.split(jax.random.key(seed), 7)
    fields = normal_values(key_of[0], (CIN, X, Y, Z), 1.0, 6.0, ((1, 8), (2, 4)))
    rows_live = draw_rows_live(jax.random.fold_in(key_of[6], 71), 0)
    cols_live = draw_cols_live(jax.random.fold_in(key_of[6], 71), 0)
    weight = normal_values(key_of[3], (COUT, CIN * 27), (CIN * 27) ** -0.5, 0.625)
    bias = normal_values(key_of[4], (COUT,), 0.5, 3.0, (), jnp.float32)
    grad_out = bell_draw_with(key_of[5], (COUT, X2, Y2, Z2), (4.0 / (X2 * Y2 * Z2) ** 0.5), 0.0625, ((0, 4), (1, 8)), (1, 0, 8, 2.0))
    return dict(fields=fields, rows_live=rows_live, cols_live=cols_live, weight=weight, bias=bias, grad_out=grad_out)


def extend(data, border, count, dim):
    length = data.shape[dim]
    border_wide = jnp.expand_dims(border, dim)
    joined = jnp.concatenate([jnp.zeros_like(border_wide), data], axis=dim)
    shape = [1] * joined.ndim
    shape[dim] = length + 1
    places = jnp.arange(length + 1, dtype=jnp.int32).reshape(shape)
    edge_at = length - count
    kept = jnp.where(places > edge_at, joined, jnp.zeros_like(joined))
    return jnp.where(places == edge_at, border_wide, kept)


def taps(padded, axes, halves):
    pieces = []
    for off_x in range(3):
        for off_y in range(3):
            for off_z in range(3):
                piece = padded
                for axis_no, offset, half in zip(axes, (off_x, off_y, off_z), halves):
                    piece = lax.slice_in_dim(piece, offset, offset + 2 * half - 1, 2, axis_no)
                pieces.append(piece)
    return pieces


def reference(fields, rows_live, cols_live, weight, bias, grad_out):
    half_x = CAPX // 2
    half_y = CAPY // 2
    half_z = Z // 2
    grid = fields.reshape(CIN, N_GX, CAPX, N_GY, CAPY, Z)
    last_rows = grid[:, :, CAPX - 1]
    above = jnp.concatenate([jnp.zeros_like(last_rows[:, :1]), last_rows[:, :-1]], axis=1)
    ext_rows = extend(grid, above, rows_live.reshape(1, N_GX, 1, 1, 1, 1), 2)
    last_cols = ext_rows[:, :, :, :, CAPY - 1]
    beside = jnp.concatenate([jnp.zeros_like(last_cols[:, :, :, :1]), last_cols[:, :, :, :-1]], axis=3)
    ext_full = extend(ext_rows, beside, cols_live.reshape(1, 1, 1, N_GY, 1, 1), 4)
    padded = jnp.pad(ext_full, ((0, 0), (0, 0), (0, 0), (0, 0), (0, 0), (1, 0)))
    row_ok = jnp.arange(half_x, dtype=jnp.int32)[None, :] >= half_x - (rows_live // 2)[:, None]
    col_ok = jnp.arange(half_y, dtype=jnp.int32)[None, :] >= half_y - (cols_live // 2)[:, None]
    live = row_ok[:, :, None, None] & col_ok[None, None, :, :]

    def row_taps(index):
        row = lax.dynamic_index_in_dim(padded, index, 1, keepdims=False)
        return jnp.stack(taps(row, (1, 3, 4), (half_x, half_y, half_z)), axis=1).reshape(CIN * 27, -1)

    def forward_row(index):
        conv = jnp.dot(weight, row_taps(index), preferred_element_type=jnp.float32) + bias[:, None]
        keep = lax.dynamic_index_in_dim(live, index, 0, keepdims=False)
        conv = conv.reshape(COUT, half_x, N_GY, half_y, half_z)
        return jnp.where(keep.reshape(1, half_x, N_GY, half_y, 1), conv, 0.0).astype(jnp.bfloat16)

    indices = jnp.arange(N_GX, dtype=jnp.int32)
    pre_rows = lax.map(forward_row, indices)
    pre = jnp.moveaxis(pre_rows, 0, 1).reshape(COUT, X2, Y2, Z2)
    pre_wide = pre.astype(jnp.float32)
    sigma = jax.nn.sigmoid(pre_wide)
    stem = (pre_wide * sigma).astype(jnp.bfloat16)
    slope = sigma * (1.0 + pre_wide * (1.0 - sigma))
    live_all = live.reshape(1, X2, Y2, 1)
    grad_pre = jnp.where(live_all, grad_out.astype(jnp.float32) * slope, 0.0).astype(jnp.bfloat16)
    grad_rows = grad_pre.reshape(COUT, N_GX, half_x, N_GY, half_y, half_z)

    def backward_row(carry, index):
        grad_row = lax.dynamic_index_in_dim(grad_rows, index, 1, keepdims=False).reshape(COUT, -1)
        patches = row_taps(index)
        part = lax.dot_general(grad_row, patches, (((1,), (1,)), ((), ())), preferred_element_type=jnp.float32)
        total = jnp.sum(grad_row.astype(jnp.float32), axis=1)
        return (carry[0] + part, carry[1] + total), None

    start = (jnp.zeros((COUT, CIN * 27), jnp.float32), jnp.zeros((COUT,), jnp.float32))
    (weight_grad, bias_grad), unused = lax.scan(backward_row, start, indices)
    return stem, weight_grad, bias_grad
```

```python
import jax
import jax.numpy as jnp
from jax import lax
from jax.sharding import PartitionSpec as P


def from_behind(block, axis, distance):
    devices = range(lax.axis_size(axis))
    route = [(i - distance, i) for i in devices if i - distance in devices]
    return lax.ppermute(block, axis, route)


def extend(data, border, count, dim):
    length = data.shape[dim]
    border_wide = jnp.expand_dims(border, dim)
    joined = jnp.concatenate([jnp.zeros_like(border_wide), data], axis=dim)
    shape = [1] * joined.ndim
    shape[dim] = length + 1
    places = jnp.arange(length + 1, dtype=jnp.int32).reshape(shape)
    edge_at = length - count
    kept = jnp.where(places > edge_at, joined, jnp.zeros_like(joined))
    return jnp.where(places == edge_at, border_wide, kept)


def taps(padded, axes, halves):
    pieces = []
    for off_x in range(3):
        for off_y in range(3):
            for off_z in range(3):
                piece = padded
                for axis_no, offset, half in zip(axes, (off_x, off_y, off_z), halves):
                    piece = lax.slice_in_dim(piece, offset, offset + 2 * half - 1, 2, axis_no)
                pieces.append(piece)
    return pieces


def local(fields, rows_live, cols_live, weight, bias, grad_out):
    in_chans, cap_x, cap_y, depth = fields.shape
    half_x = cap_x // 2
    half_y = cap_y // 2
    half_z = depth // 2
    out_chans = weight.shape[0]
    tiles_y = lax.axis_size("gy")
    row_count = rows_live[lax.axis_index("gx")]
    above = from_behind(fields[:, cap_x - 1], "gx", 1)
    ext_rows = extend(fields, above, row_count, 1)
    row_ok = jnp.arange(half_x, dtype=jnp.int32) >= half_x - row_count // 2
    col_count = cols_live[lax.axis_index("gy")]
    beside = from_behind(ext_rows[:, :, cap_y - 1], "gy", 1)
    ext_full = extend(ext_rows, beside, col_count, 2)
    lhs = ext_full[None]
    kernel = weight.reshape(out_chans, in_chans, 3, 3, 3)
    dims = ("NCDHW", "OIDHW", "NCDHW")
    conv = lax.conv_general_dilated(
        lhs, kernel, (2, 2, 2), ((0, 0), (0, 0), (1, 0)),
        dimension_numbers=dims, preferred_element_type=jnp.float32,
    )[0] + bias[:, None, None, None]
    col_ok = jnp.arange(half_y, dtype=jnp.int32) >= half_y - col_count // 2
    live = (row_ok[:, None] & col_ok[None, :]).reshape(1, half_x, half_y, 1)
    pre_local = jnp.where(live, conv, 0.0).astype(jnp.bfloat16)
    regrouped = lax.all_to_all(pre_local, "gy", split_axis=0, concat_axis=2, tiled=True)
    pre_wide = regrouped.astype(jnp.float32)
    sigma = jax.nn.sigmoid(pre_wide)
    stem = (pre_wide * sigma).astype(jnp.bfloat16)
    wide_cols = jnp.arange(half_y, dtype=jnp.int32)[None, :] >= half_y - (cols_live // 2)[:, None]
    wide_live = row_ok.reshape(1, half_x, 1, 1) & wide_cols.reshape(1, 1, tiles_y * half_y, 1)
    slope = sigma * (1.0 + pre_wide * (1.0 - sigma))
    grad_pre = jnp.where(wide_live, grad_out.astype(jnp.float32) * slope, 0.0).astype(jnp.bfloat16)
    returned = lax.all_to_all(grad_pre, "gy", split_axis=2, concat_axis=0, tiled=True)
    filt = lax.conv_general_dilated(
        ext_full[:, None], returned[:, None], (1, 1, 1), ((0, 0), (0, 0), (1, 0)),
        rhs_dilation=(2, 2, 2), dimension_numbers=dims,
        preferred_element_type=jnp.float32,
    )
    weight_full = jnp.swapaxes(filt, 0, 1).reshape(out_chans, -1)
    bias_full = jnp.sum(returned.astype(jnp.float32), axis=(1, 2, 3))
    packed = jnp.concatenate([weight_full, bias_full[:, None]], axis=1)
    total = lax.psum(packed, ("gx", "gy"))
    rows = out_chans // tiles_y
    mine = lax.dynamic_slice_in_dim(total, lax.axis_index("gy") * rows, rows, 0)
    weight_grad, bias_grad = mine[:, :-1], mine[:, -1]
    return (stem, weight_grad, bias_grad)


def solution(mesh):
    in_specs = (P(None, "gx", "gy", None), P(), P(), P(), P(), P("gy", "gx", None, None))
    out_specs = (P("gy", "gx", None, None), P("gy", None), P("gy"))
    return jax.shard_map(local, mesh=mesh, in_specs=in_specs, out_specs=out_specs, check_vma=False)
```

```python
import jax
import jax.numpy as jnp
from jax import lax
from jax.sharding import PartitionSpec as P


def from_behind(block, axis, distance):
    devices = range(lax.axis_size(axis))
    route = [(i - distance, i) for i in devices if i - distance in devices]
    return lax.ppermute(block, axis, route)


def extend(data, border, count, dim):
    length = data.shape[dim]
    border_wide = jnp.expand_dims(border, dim)
    joined = jnp.concatenate([jnp.zeros_like(border_wide), data], axis=dim)
    shape = [1] * joined.ndim
    shape[dim] = length + 1
    places = jnp.arange(length + 1, dtype=jnp.int32).reshape(shape)
    edge_at = length - count
    kept = jnp.where(places > edge_at, joined, jnp.zeros_like(joined))
    return jnp.where(places == edge_at, border_wide, kept)


def taps(padded, axes, halves):
    pieces = []
    for off_x in range(3):
        for off_y in range(3):
            for off_z in range(3):
                piece = padded
                for axis_no, offset, half in zip(axes, (off_x, off_y, off_z), halves):
                    piece = lax.slice_in_dim(piece, offset, offset + 2 * half - 1, 2, axis_no)
                pieces.append(piece)
    return pieces


def local(fields, rows_live, cols_live, weight, bias, grad_out):
    in_chans, cap_x, cap_y, depth = fields.shape
    half_x = cap_x // 2
    half_y = cap_y // 2
    half_z = depth // 2
    out_chans = weight.shape[0]
    tiles_y = lax.axis_size("gy")
    row_count = rows_live[lax.axis_index("gx")]
    above = from_behind(fields[:, cap_x - 1], "gx", 1)
    ext_rows = extend(fields, above, row_count, 1)
    row_ok = jnp.arange(half_x, dtype=jnp.int32) >= half_x - row_count // 2
    col_count = cols_live[lax.axis_index("gy")]
    beside = from_behind(ext_rows[:, :, cap_y - 1], "gy", 1)
    ext_full = extend(ext_rows, beside, col_count, 2)
    lanes = jnp.arange(3 * half_z, dtype=jnp.int32)
    source = 2 * (lanes % half_z) + lanes // half_z - 1
    pick = (jnp.arange(depth, dtype=jnp.int32)[:, None] == source[None, :]).astype(fields.dtype)
    ztaps = jnp.einsum("cxyz,zk->cxyk", ext_full, pick, preferred_element_type=jnp.float32)
    ztaps = ztaps.astype(fields.dtype)
    blocks = []
    for off_x in range(3):
        for off_y in range(3):
            blocks.append(ztaps[:, off_x : off_x + 2 * half_x - 1 : 2, off_y : off_y + 2 * half_y - 1 : 2])
    stacked = jnp.stack(blocks, axis=1).reshape(in_chans * 9, half_x, half_y, 3 * half_z)
    kernel = weight.reshape(out_chans, in_chans * 9, 3)
    conv = bias[:, None, None, None]
    for off_z in range(3):
        part = stacked[..., off_z * half_z : (off_z + 1) * half_z]
        conv = conv + jnp.einsum("ok,kpqr->opqr", kernel[:, :, off_z], part, preferred_element_type=jnp.float32)
    col_ok = jnp.arange(half_y, dtype=jnp.int32) >= half_y - col_count // 2
    live = (row_ok[:, None] & col_ok[None, :]).reshape(1, half_x, half_y, 1)
    pre_local = jnp.where(live, conv, 0.0).astype(jnp.bfloat16)
    regrouped = lax.all_to_all(pre_local, "gy", split_axis=0, concat_axis=2, tiled=True)
    pre_wide = regrouped.astype(jnp.float32)
    sigma = jax.nn.sigmoid(pre_wide)
    stem = (pre_wide * sigma).astype(jnp.bfloat16)
    wide_cols = jnp.arange(half_y, dtype=jnp.int32)[None, :] >= half_y - (cols_live // 2)[:, None]
    wide_live = row_ok.reshape(1, half_x, 1, 1) & wide_cols.reshape(1, 1, tiles_y * half_y, 1)
    slope = sigma * (1.0 + pre_wide * (1.0 - sigma))
    grad_pre = jnp.where(wide_live, grad_out.astype(jnp.float32) * slope, 0.0).astype(jnp.bfloat16)
    returned = lax.all_to_all(grad_pre, "gy", split_axis=2, concat_axis=0, tiled=True)
    grads = []
    for off_z in range(3):
        part = stacked[..., off_z * half_z : (off_z + 1) * half_z]
        grads.append(jnp.einsum("opqr,kpqr->ok", returned, part, preferred_element_type=jnp.float32))
    weight_full = jnp.stack(grads, axis=-1).reshape(out_chans, -1)
    bias_full = jnp.sum(returned.astype(jnp.float32), axis=(1, 2, 3))
    weight_part, bias_part = (
        lax.psum_scatter(weight_full, "gy", scatter_dimension=0, tiled=True),
        lax.psum_scatter(bias_full, "gy", scatter_dimension=0, tiled=True),
    )
    weight_grad, bias_grad = lax.psum((weight_part, bias_part), "gx")
    return (stem, weight_grad, bias_grad)


def solution(mesh):
    in_specs = (P(None, "gx", "gy", None), P(), P(), P(), P(), P("gy", "gx", None, None))
    out_specs = (P("gy", "gx", None, None), P("gy", None), P("gy"))
    return jax.shard_map(local, mesh=mesh, in_specs=in_specs, out_specs=out_specs, check_vma=False)
```

```python
import jax
import jax.numpy as jnp
from jax import lax
from jax.sharding import PartitionSpec as P


def from_behind(block, axis, distance):
    devices = range(lax.axis_size(axis))
    route = [(i - distance, i) for i in devices if i - distance in devices]
    return lax.ppermute(block, axis, route)


def butterfly_sum(value, axis):
    size = lax.axis_size(axis)
    if size & (size - 1):
        return lax.psum(value, axis)
    step = 1
    while step < size:
        swap = [(i, i ^ step) for i in range(size)]
        value = value + lax.ppermute(value, axis, swap)
        step *= 2
    return value


def extend(data, border, count, dim):
    length = data.shape[dim]
    border_wide = jnp.expand_dims(border, dim)
    joined = jnp.concatenate([jnp.zeros_like(border_wide), data], axis=dim)
    shape = [1] * joined.ndim
    shape[dim] = length + 1
    places = jnp.arange(length + 1, dtype=jnp.int32).reshape(shape)
    edge_at = length - count
    kept = jnp.where(places > edge_at, joined, jnp.zeros_like(joined))
    return jnp.where(places == edge_at, border_wide, kept)


def taps(padded, axes, halves):
    pieces = []
    for off_x in range(3):
        for off_y in range(3):
            for off_z in range(3):
                piece = padded
                for axis_no, offset, half in zip(axes, (off_x, off_y, off_z), halves):
                    piece = lax.slice_in_dim(piece, offset, offset + 2 * half - 1, 2, axis_no)
                pieces.append(piece)
    return pieces


def local(fields, rows_live, cols_live, weight, bias, grad_out):
    in_chans, cap_x, cap_y, depth = fields.shape
    half_x = cap_x // 2
    half_y = cap_y // 2
    half_z = depth // 2
    out_chans = weight.shape[0]
    tiles_y = lax.axis_size("gy")
    row_count = rows_live[lax.axis_index("gx")]
    above = from_behind(fields[:, cap_x - 1], "gx", 1)
    ext_rows = extend(fields, above, row_count, 1)
    row_ok = jnp.arange(half_x, dtype=jnp.int32) >= half_x - row_count // 2
    col_count = cols_live[lax.axis_index("gy")]
    beside = from_behind(ext_rows[:, :, cap_y - 1], "gy", 1)
    ext_full = extend(ext_rows, beside, col_count, 2)
    lanes = jnp.arange(3 * half_z, dtype=jnp.int32)
    source = 2 * (lanes % half_z) + lanes // half_z - 1
    pick = (jnp.arange(depth, dtype=jnp.int32)[:, None] == source[None, :]).astype(fields.dtype)
    ztaps = jnp.einsum("cxyz,zk->cxyk", ext_full, pick, preferred_element_type=jnp.float32)
    ztaps = ztaps.astype(fields.dtype)
    blocks = []
    for off_x in range(3):
        for off_y in range(3):
            blocks.append(ztaps[:, off_x : off_x + 2 * half_x - 1 : 2, off_y : off_y + 2 * half_y - 1 : 2])
    stacked = jnp.stack(blocks, axis=1).reshape(in_chans * 9, half_x, half_y, 3 * half_z)
    kernel = weight.reshape(out_chans, in_chans * 9, 3)
    conv = bias[:, None, None, None]
    for off_z in range(3):
        part = stacked[..., off_z * half_z : (off_z + 1) * half_z]
        conv = conv + jnp.einsum("ok,kpqr->opqr", kernel[:, :, off_z], part, preferred_element_type=jnp.float32)
    col_ok = jnp.arange(half_y, dtype=jnp.int32) >= half_y - col_count // 2
    live = (row_ok[:, None] & col_ok[None, :]).reshape(1, half_x, half_y, 1)
    pre_local = jnp.where(live, conv, 0.0).astype(jnp.bfloat16)
    regrouped = lax.all_to_all(pre_local, "gy", split_axis=0, concat_axis=2, tiled=True)
    pre_wide = regrouped.astype(jnp.float32)
    sigma = jax.nn.sigmoid(pre_wide)
    stem = (pre_wide * sigma).astype(jnp.bfloat16)
    wide_cols = jnp.arange(half_y, dtype=jnp.int32)[None, :] >= half_y - (cols_live // 2)[:, None]
    wide_live = row_ok.reshape(1, half_x, 1, 1) & wide_cols.reshape(1, 1, tiles_y * half_y, 1)
    slope = sigma * (1.0 + pre_wide * (1.0 - sigma))
    grad_pre = jnp.where(wide_live, grad_out.astype(jnp.float32) * slope, 0.0).astype(jnp.bfloat16)
    returned = lax.all_to_all(grad_pre, "gy", split_axis=2, concat_axis=0, tiled=True)
    grads = []
    for off_z in range(3):
        part = stacked[..., off_z * half_z : (off_z + 1) * half_z]
        grads.append(jnp.einsum("opqr,kpqr->ok", returned, part, preferred_element_type=jnp.float32))
    weight_full = jnp.stack(grads, axis=-1).reshape(out_chans, -1)
    bias_full = jnp.sum(returned.astype(jnp.float32), axis=(1, 2, 3))
    packed = jnp.concatenate([weight_full, bias_full[:, None]], axis=1)
    total = butterfly_sum(butterfly_sum(packed, "gx"), "gy")
    rows = out_chans // tiles_y
    mine = lax.dynamic_slice_in_dim(total, lax.axis_index("gy") * rows, rows, 0)
    weight_grad, bias_grad = mine[:, :-1], mine[:, -1]
    return (stem, weight_grad, bias_grad)


def solution(mesh):
    in_specs = (P(None, "gx", "gy", None), P(), P(), P(), P(), P("gy", "gx", None, None))
    out_specs = (P("gy", "gx", None, None), P("gy", None), P("gy"))
    return jax.shard_map(local, mesh=mesh, in_specs=in_specs, out_specs=out_specs, check_vma=False)
```

```python
import jax
import jax.numpy as jnp
from jax import lax
from jax.sharding import PartitionSpec as P


def from_behind(block, axis, distance):
    devices = range(lax.axis_size(axis))
    route = [(i - distance, i) for i in devices if i - distance in devices]
    return lax.ppermute(block, axis, route)


def butterfly_sum(value, axis):
    size = lax.axis_size(axis)
    if size & (size - 1):
        return lax.psum(value, axis)
    step = 1
    while step < size:
        swap = [(i, i ^ step) for i in range(size)]
        value = value + lax.ppermute(value, axis, swap)
        step *= 2
    return value


def extend(data, border, count, dim):
    length = data.shape[dim]
    border_wide = jnp.expand_dims(border, dim)
    joined = jnp.concatenate([jnp.zeros_like(border_wide), data], axis=dim)
    shape = [1] * joined.ndim
    shape[dim] = length + 1
    places = jnp.arange(length + 1, dtype=jnp.int32).reshape(shape)
    edge_at = length - count
    kept = jnp.where(places > edge_at, joined, jnp.zeros_like(joined))
    return jnp.where(places == edge_at, border_wide, kept)


def taps(padded, axes, halves):
    pieces = []
    for off_x in range(3):
        for off_y in range(3):
            for off_z in range(3):
                piece = padded
                for axis_no, offset, half in zip(axes, (off_x, off_y, off_z), halves):
                    piece = lax.slice_in_dim(piece, offset, offset + 2 * half - 1, 2, axis_no)
                pieces.append(piece)
    return pieces


def local(fields, rows_live, cols_live, weight, bias, grad_out):
    in_chans, cap_x, cap_y, depth = fields.shape
    half_x = cap_x // 2
    half_y = cap_y // 2
    half_z = depth // 2
    out_chans = weight.shape[0]
    tiles_y = lax.axis_size("gy")
    cell_grad = lax.all_to_all(grad_out, "gy", split_axis=2, concat_axis=0, tiled=True)
    row_count = rows_live[lax.axis_index("gx")]
    above = from_behind(fields[:, cap_x - 1], "gx", 1)
    ext_rows = extend(fields, above, row_count, 1)
    row_ok = jnp.arange(half_x, dtype=jnp.int32) >= half_x - row_count // 2
    col_count = cols_live[lax.axis_index("gy")]
    beside = from_behind(ext_rows[:, :, cap_y - 1], "gy", 1)
    ext_full = extend(ext_rows, beside, col_count, 2)
    lanes = jnp.arange(3 * half_z, dtype=jnp.int32)
    source = 2 * (lanes % half_z) + lanes // half_z - 1
    pick = (jnp.arange(depth, dtype=jnp.int32)[:, None] == source[None, :]).astype(fields.dtype)
    ztaps = jnp.einsum("cxyz,zk->cxyk", ext_full, pick, preferred_element_type=jnp.float32)
    ztaps = ztaps.astype(fields.dtype)
    blocks = []
    for off_x in range(3):
        for off_y in range(3):
            blocks.append(ztaps[:, off_x : off_x + 2 * half_x - 1 : 2, off_y : off_y + 2 * half_y - 1 : 2])
    stacked = jnp.stack(blocks, axis=1).reshape(in_chans * 9, half_x, half_y, 3 * half_z)
    kernel = weight.reshape(out_chans, in_chans * 9, 3)
    conv = bias[:, None, None, None]
    for off_z in range(3):
        part = stacked[..., off_z * half_z : (off_z + 1) * half_z]
        conv = conv + jnp.einsum("ok,kpqr->opqr", kernel[:, :, off_z], part, preferred_element_type=jnp.float32)
    col_ok = jnp.arange(half_y, dtype=jnp.int32) >= half_y - col_count // 2
    live = (row_ok[:, None] & col_ok[None, :]).reshape(1, half_x, half_y, 1)
    pre_local = jnp.where(live, conv, 0.0).astype(jnp.bfloat16)
    pre_wide = pre_local.astype(jnp.float32)
    sigma = jax.nn.sigmoid(pre_wide)
    stem_local = (pre_wide * sigma).astype(jnp.bfloat16)
    slope = sigma * (1.0 + pre_wide * (1.0 - sigma))
    returned = jnp.where(live, cell_grad.astype(jnp.float32) * slope, 0.0).astype(jnp.bfloat16)
    stem = lax.all_to_all(stem_local, "gy", split_axis=0, concat_axis=2, tiled=True)
    grads = []
    for off_z in range(3):
        part = stacked[..., off_z * half_z : (off_z + 1) * half_z]
        grads.append(jnp.einsum("opqr,kpqr->ok", returned, part, preferred_element_type=jnp.float32))
    weight_full = jnp.stack(grads, axis=-1).reshape(out_chans, -1)
    bias_full = jnp.sum(returned.astype(jnp.float32), axis=(1, 2, 3))
    packed = jnp.concatenate([weight_full, bias_full[:, None]], axis=1)
    total = butterfly_sum(butterfly_sum(packed, "gx"), "gy")
    rows = out_chans // tiles_y
    mine = lax.dynamic_slice_in_dim(total, lax.axis_index("gy") * rows, rows, 0)
    weight_grad, bias_grad = mine[:, :-1], mine[:, -1]
    return (stem, weight_grad, bias_grad)


def solution(mesh):
    in_specs = (P(None, "gx", "gy", None), P(), P(), P(), P(), P("gy", "gx", None, None))
    out_specs = (P("gy", "gx", None, None), P("gy", None), P("gy"))
    return jax.shard_map(local, mesh=mesh, in_specs=in_specs, out_specs=out_specs, check_vma=False)
```

```python
import jax
import jax.numpy as jnp
from jax import lax
from jax.sharding import PartitionSpec as P


def from_behind(block, axis, distance):
    devices = range(lax.axis_size(axis))
    route = [(i - distance, i) for i in devices if i - distance in devices]
    return lax.ppermute(block, axis, route)


def butterfly_sum(value, axis):
    size = lax.axis_size(axis)
    if size & (size - 1):
        return lax.psum(value, axis)
    step = 1
    while step < size:
        swap = [(i, i ^ step) for i in range(size)]
        value = value + lax.ppermute(value, axis, swap)
        step *= 2
    return value


def extend(data, border, count, dim):
    length = data.shape[dim]
    border_wide = jnp.expand_dims(border, dim)
    joined = jnp.concatenate([jnp.zeros_like(border_wide), data], axis=dim)
    shape = [1] * joined.ndim
    shape[dim] = length + 1
    places = jnp.arange(length + 1, dtype=jnp.int32).reshape(shape)
    edge_at = length - count
    kept = jnp.where(places > edge_at, joined, jnp.zeros_like(joined))
    return jnp.where(places == edge_at, border_wide, kept)


def taps(padded, axes, halves):
    pieces = []
    for off_x in range(3):
        for off_y in range(3):
            for off_z in range(3):
                piece = padded
                for axis_no, offset, half in zip(axes, (off_x, off_y, off_z), halves):
                    piece = lax.slice_in_dim(piece, offset, offset + 2 * half - 1, 2, axis_no)
                pieces.append(piece)
    return pieces


def local(fields, rows_live, cols_live, weight, bias, grad_out):
    in_chans, cap_x, cap_y, depth = fields.shape
    half_x = cap_x // 2
    half_y = cap_y // 2
    half_z = depth // 2
    out_chans = weight.shape[0]
    tiles_y = lax.axis_size("gy")
    cell_grad = lax.all_to_all(grad_out, "gy", split_axis=2, concat_axis=0, tiled=True)
    row_count = rows_live[lax.axis_index("gx")]
    above = from_behind(fields[:, cap_x - 1], "gx", 1)
    ext_rows = extend(fields, above, row_count, 1)
    row_ok = jnp.arange(half_x, dtype=jnp.int32) >= half_x - row_count // 2
    col_count = cols_live[lax.axis_index("gy")]
    beside = from_behind(ext_rows[:, :, cap_y - 1], "gy", 1)
    ext_full = extend(ext_rows, beside, col_count, 2)
    lanes = jnp.arange(3 * half_z, dtype=jnp.int32)
    source = 2 * (lanes % half_z) + lanes // half_z - 1
    pick = (jnp.arange(depth, dtype=jnp.int32)[:, None] == source[None, :]).astype(fields.dtype)
    ztaps = jnp.einsum("cxyz,zk->cxyk", ext_full, pick, preferred_element_type=jnp.float32)
    ztaps = ztaps.astype(fields.dtype)
    blocks = []
    for off_x in range(3):
        for off_y in range(3):
            blocks.append(ztaps[:, off_x : off_x + 2 * half_x - 1 : 2, off_y : off_y + 2 * half_y - 1 : 2])
    stacked = jnp.stack(blocks, axis=1).reshape(in_chans * 9, half_x, half_y, 3 * half_z)
    kernel = weight.reshape(out_chans, in_chans * 9, 3)
    conv = bias[:, None, None, None]
    for off_z in range(3):
        part = stacked[..., off_z * half_z : (off_z + 1) * half_z]
        conv = conv + jnp.einsum("ok,kpqr->opqr", kernel[:, :, off_z], part, preferred_element_type=jnp.float32)
    col_ok = jnp.arange(half_y, dtype=jnp.int32) >= half_y - col_count // 2
    live = (row_ok[:, None] & col_ok[None, :]).reshape(1, half_x, half_y, 1)
    pre_wide = lax.reduce_precision(jnp.where(live, conv, 0.0), exponent_bits=8, mantissa_bits=7)
    sigma = jax.nn.sigmoid(pre_wide)
    stem_local = (pre_wide * sigma).astype(jnp.bfloat16)
    slope = sigma * (1.0 + pre_wide * (1.0 - sigma))
    returned = jnp.where(live, cell_grad.astype(jnp.float32) * slope, 0.0).astype(jnp.bfloat16)
    stem = lax.all_to_all(stem_local, "gy", split_axis=0, concat_axis=2, tiled=True)
    grads = []
    for off_z in range(3):
        part = stacked[..., off_z * half_z : (off_z + 1) * half_z]
        grads.append(jnp.einsum("opqr,kpqr->ok", returned, part, preferred_element_type=jnp.float32))
    weight_full = jnp.stack(grads, axis=-1).reshape(out_chans, -1)
    bias_full = jnp.sum(returned.astype(jnp.float32), axis=(1, 2, 3))
    packed = jnp.concatenate([weight_full, bias_full[:, None]], axis=1)
    total = butterfly_sum(butterfly_sum(packed, "gx"), "gy")
    rows = out_chans // tiles_y
    mine = lax.dynamic_slice_in_dim(total, lax.axis_index("gy") * rows, rows, 0)
    weight_grad, bias_grad = mine[:, :-1], mine[:, -1]
    return (stem, weight_grad, bias_grad)


def solution(mesh):
    in_specs = (P(None, "gx", "gy", None), P(), P(), P(), P(), P("gy", "gx", None, None))
    out_specs = (P("gy", "gx", None, None), P("gy", None), P("gy"))
    return jax.shard_map(local, mesh=mesh, in_specs=in_specs, out_specs=out_specs, check_vma=False)
```

```python
import jax
import jax.numpy as jnp
from jax import lax
from jax.sharding import PartitionSpec as P


def from_behind(block, axis, distance):
    devices = range(lax.axis_size(axis))
    route = [(i - distance, i) for i in devices if i - distance in devices]
    return lax.ppermute(block, axis, route)


def from_diagonal(block):
    nx, ny = lax.axis_size("gx"), lax.axis_size("gy")
    route = [((i - 1) * ny + j - 1, i * ny + j) for i in range(1, nx) for j in range(1, ny)]
    return lax.ppermute(block, ("gx", "gy"), route)


def pick_count(counts, axis):
    here = jnp.arange(counts.shape[0], dtype=jnp.int32) == lax.axis_index(axis)
    return jnp.sum(jnp.where(here, counts, 0))


def butterfly_sum(value, axis):
    size = lax.axis_size(axis)
    if size & (size - 1):
        return lax.psum(value, axis)
    step = 1
    while step < size:
        swap = [(i, i ^ step) for i in range(size)]
        value = value + lax.ppermute(value, axis, swap)
        step *= 2
    return value


def extend(data, border, count, dim):
    length = data.shape[dim]
    border_wide = jnp.expand_dims(border, dim)
    joined = jnp.concatenate([jnp.zeros_like(border_wide), data], axis=dim)
    shape = [1] * joined.ndim
    shape[dim] = length + 1
    places = jnp.arange(length + 1, dtype=jnp.int32).reshape(shape)
    edge_at = length - count
    kept = jnp.where(places > edge_at, joined, jnp.zeros_like(joined))
    return jnp.where(places == edge_at, border_wide, kept)


def taps(padded, axes, halves):
    pieces = []
    for off_x in range(3):
        for off_y in range(3):
            for off_z in range(3):
                piece = padded
                for axis_no, offset, half in zip(axes, (off_x, off_y, off_z), halves):
                    piece = lax.slice_in_dim(piece, offset, offset + 2 * half - 1, 2, axis_no)
                pieces.append(piece)
    return pieces


def local(fields, rows_live, cols_live, weight, bias, grad_out):
    in_chans, cap_x, cap_y, depth = fields.shape
    half_x = cap_x // 2
    half_y = cap_y // 2
    half_z = depth // 2
    out_chans = weight.shape[0]
    tiles_y = lax.axis_size("gy")
    cell_grad = lax.all_to_all(grad_out, "gy", split_axis=2, concat_axis=0, tiled=True)
    row_count = pick_count(rows_live, "gx")
    col_count = pick_count(cols_live, "gy")
    above = from_behind(fields[:, cap_x - 1], "gx", 1)
    side = from_behind(fields[:, :, cap_y - 1], "gy", 1)
    corner = from_diagonal(fields[:, cap_x - 1, cap_y - 1])
    ext_rows = extend(fields, above, row_count, 1)
    beside = extend(side, corner, row_count, 1)
    row_ok = jnp.arange(half_x, dtype=jnp.int32) >= half_x - row_count // 2
    ext_full = extend(ext_rows, beside, col_count, 2)
    lanes = jnp.arange(3 * half_z, dtype=jnp.int32)
    source = 2 * (lanes % half_z) + lanes // half_z - 1
    pick = (jnp.arange(depth, dtype=jnp.int32)[:, None] == source[None, :]).astype(fields.dtype)
    ztaps = jnp.einsum("cxyz,zk->cxyk", ext_full, pick, preferred_element_type=jnp.float32)
    ztaps = ztaps.astype(fields.dtype)
    blocks = []
    for off_x in range(3):
        for off_y in range(3):
            blocks.append(ztaps[:, off_x : off_x + 2 * half_x - 1 : 2, off_y : off_y + 2 * half_y - 1 : 2])
    stacked = jnp.stack(blocks, axis=1).reshape(in_chans * 9, half_x, half_y, 3 * half_z)
    kernel = weight.reshape(out_chans, in_chans * 9, 3)
    conv = bias[:, None, None, None]
    for off_z in range(3):
        part = stacked[..., off_z * half_z : (off_z + 1) * half_z]
        conv = conv + jnp.einsum("ok,kpqr->opqr", kernel[:, :, off_z], part, preferred_element_type=jnp.float32)
    col_ok = jnp.arange(half_y, dtype=jnp.int32) >= half_y - col_count // 2
    live = (row_ok[:, None] & col_ok[None, :]).reshape(1, half_x, half_y, 1)
    pre_wide = lax.reduce_precision(jnp.where(live, conv, 0.0), exponent_bits=8, mantissa_bits=7)
    sigma = jax.nn.sigmoid(pre_wide)
    stem_local = (pre_wide * sigma).astype(jnp.bfloat16)
    slope = sigma * (1.0 + pre_wide * (1.0 - sigma))
    grad_wide = jnp.where(live, cell_grad.astype(jnp.float32) * slope, 0.0)
    grad_wide = lax.reduce_precision(grad_wide, exponent_bits=8, mantissa_bits=7)
    returned = grad_wide.astype(jnp.bfloat16)
    stem = lax.all_to_all(stem_local, "gy", split_axis=0, concat_axis=2, tiled=True)
    grads = []
    for off_z in range(3):
        part = stacked[..., off_z * half_z : (off_z + 1) * half_z]
        grads.append(jnp.einsum("opqr,kpqr->ok", returned, part, preferred_element_type=jnp.float32))
    weight_full = jnp.stack(grads, axis=-1).reshape(out_chans, -1)
    bias_full = jnp.sum(grad_wide, axis=(1, 2, 3))
    packed = jnp.concatenate([weight_full, bias_full[:, None]], axis=1)
    total = butterfly_sum(butterfly_sum(packed, "gx"), "gy")
    rows = out_chans // tiles_y
    mine = lax.dynamic_slice_in_dim(total, lax.axis_index("gy") * rows, rows, 0)
    weight_grad, bias_grad = mine[:, :-1], mine[:, -1]
    return (stem, weight_grad, bias_grad)


def solution(mesh):
    in_specs = (P(None, "gx", "gy", None), P(), P(), P(), P(), P("gy", "gx", None, None))
    out_specs = (P("gy", "gx", None, None), P("gy", None), P("gy"))
    return jax.shard_map(local, mesh=mesh, in_specs=in_specs, out_specs=out_specs, check_vma=False)
```

```python
import jax
import jax.numpy as jnp
from jax import lax
from jax.sharding import PartitionSpec as P


def from_behind(block, axis, distance):
    devices = range(lax.axis_size(axis))
    route = [(i - distance, i) for i in devices if i - distance in devices]
    return lax.ppermute(block, axis, route)


def butterfly_sum(value, axis):
    size = lax.axis_size(axis)
    if size & (size - 1):
        return lax.psum(value, axis)
    step = 1
    while step < size:
        swap = [(i, i ^ step) for i in range(size)]
        value = value + lax.ppermute(value, axis, swap)
        step *= 2
    return value


def extend(data, border, keep, at, dim):
    length = data.shape[dim]
    border_wide = jnp.expand_dims(border, dim)
    joined = jnp.concatenate([jnp.zeros_like(border_wide), data], axis=dim)
    shape = [1] * joined.ndim
    shape[dim] = length + 1
    kept = jnp.where(keep.reshape(shape), joined, jnp.zeros_like(joined))
    return jnp.where(at.reshape(shape), border_wide, kept)


def count_masks(counts, axis, length):
    here = (jnp.arange(counts.shape[0], dtype=jnp.int32) == lax.axis_index(axis))[:, None]
    places = jnp.arange(length + 1, dtype=jnp.int32)[None, :]
    edge = (length - counts)[:, None]
    keep = jnp.any(here & (places > edge), axis=0)
    at = jnp.any(here & (places == edge), axis=0)
    half = jnp.arange(length // 2, dtype=jnp.int32)[None, :]
    ok = jnp.any(here & (half >= length // 2 - (counts // 2)[:, None]), axis=0)
    return keep, at, ok


def taps(padded, axes, halves):
    pieces = []
    for off_x in range(3):
        for off_y in range(3):
            for off_z in range(3):
                piece = padded
                for axis_no, offset, half in zip(axes, (off_x, off_y, off_z), halves):
                    piece = lax.slice_in_dim(piece, offset, offset + 2 * half - 1, 2, axis_no)
                pieces.append(piece)
    return pieces


def local(fields, rows_live, cols_live, weight, bias, grad_out):
    in_chans, cap_x, cap_y, depth = fields.shape
    half_x = cap_x // 2
    half_y = cap_y // 2
    half_z = depth // 2
    out_chans = weight.shape[0]
    tiles_y = lax.axis_size("gy")
    cell_grad = lax.all_to_all(grad_out, "gy", split_axis=2, concat_axis=0, tiled=True)
    row_keep, row_at, row_ok = count_masks(rows_live, "gx", cap_x)
    col_keep, col_at, col_ok = count_masks(cols_live, "gy", cap_y)
    above = from_behind(fields[:, cap_x - 1], "gx", 1)
    ext_rows = extend(fields, above, row_keep, row_at, 1)
    beside = from_behind(ext_rows[:, :, cap_y - 1], "gy", 1)
    ext_full = extend(ext_rows, beside, col_keep, col_at, 2)
    lanes = jnp.arange(3 * half_z, dtype=jnp.int32)
    source = 2 * (lanes % half_z) + lanes // half_z - 1
    pick = (jnp.arange(depth, dtype=jnp.int32)[:, None] == source[None, :]).astype(fields.dtype)
    ztaps = jnp.einsum("cxyz,zk->cxyk", ext_full, pick, preferred_element_type=jnp.float32)
    ztaps = ztaps.astype(fields.dtype)
    blocks = []
    for off_x in range(3):
        for off_y in range(3):
            blocks.append(ztaps[:, off_x : off_x + 2 * half_x - 1 : 2, off_y : off_y + 2 * half_y - 1 : 2])
    stacked = jnp.stack(blocks, axis=1).reshape(in_chans * 9, half_x, half_y, 3 * half_z)
    kernel = weight.reshape(out_chans, in_chans * 9, 3)
    conv = bias[:, None, None, None]
    for off_z in range(3):
        part = stacked[..., off_z * half_z : (off_z + 1) * half_z]
        conv = conv + jnp.einsum("ok,kpqr->opqr", kernel[:, :, off_z], part, preferred_element_type=jnp.float32)
    live = (row_ok[:, None] & col_ok[None, :]).reshape(1, half_x, half_y, 1)
    pre_wide = lax.reduce_precision(jnp.where(live, conv, 0.0), exponent_bits=8, mantissa_bits=7)
    sigma = jax.nn.sigmoid(pre_wide)
    stem_local = (pre_wide * sigma).astype(jnp.bfloat16)
    slope = sigma * (1.0 + pre_wide * (1.0 - sigma))
    grad_wide = jnp.where(live, cell_grad.astype(jnp.float32) * slope, 0.0)
    grad_wide = lax.reduce_precision(grad_wide, exponent_bits=8, mantissa_bits=7)
    returned = grad_wide.astype(jnp.bfloat16)
    stem = lax.all_to_all(stem_local, "gy", split_axis=0, concat_axis=2, tiled=True)
    grads = []
    for off_z in range(3):
        part = stacked[..., off_z * half_z : (off_z + 1) * half_z]
        grads.append(jnp.einsum("opqr,kpqr->ok", returned, part, preferred_element_type=jnp.float32))
    weight_full = jnp.stack(grads, axis=-1).reshape(out_chans, -1)
    bias_full = jnp.sum(grad_wide, axis=(1, 2, 3))
    packed = jnp.concatenate([weight_full, bias_full[:, None]], axis=1)
    total = butterfly_sum(butterfly_sum(packed, "gx"), "gy")
    rows = out_chans // tiles_y
    mine = lax.dynamic_slice_in_dim(total, lax.axis_index("gy") * rows, rows, 0)
    weight_grad, bias_grad = mine[:, :-1], mine[:, -1]
    return (stem, weight_grad, bias_grad)


def solution(mesh):
    in_specs = (P(None, "gx", "gy", None), P(), P(), P(), P(), P("gy", "gx", None, None))
    out_specs = (P("gy", "gx", None, None), P("gy", None), P("gy"))
    return jax.shard_map(local, mesh=mesh, in_specs=in_specs, out_specs=out_specs, check_vma=False)
```

```python
import jax
import jax.numpy as jnp
from jax import lax
from jax.sharding import PartitionSpec as P


def from_behind(block, axis, distance):
    devices = range(lax.axis_size(axis))
    route = [(i - distance, i) for i in devices if i - distance in devices]
    return lax.ppermute(block, axis, route)


def butterfly_sum(value, axis):
    size = lax.axis_size(axis)
    if size & (size - 1):
        return lax.psum(value, axis)
    step = 1
    while step < size:
        swap = [(i, i ^ step) for i in range(size)]
        value = value + lax.ppermute(value, axis, swap)
        step *= 2
    return value


def extend(data, border, keep, at, dim):
    length = data.shape[dim]
    border_wide = jnp.expand_dims(border, dim)
    joined = jnp.concatenate([jnp.zeros_like(border_wide), data], axis=dim)
    shape = [1] * joined.ndim
    shape[dim] = length + 1
    kept = jnp.where(keep.reshape(shape), joined, jnp.zeros_like(joined))
    return jnp.where(at.reshape(shape), border_wide, kept)


def count_masks(counts, axis, length):
    here = (jnp.arange(counts.shape[0], dtype=jnp.int32) == lax.axis_index(axis))[:, None]
    places = jnp.arange(length + 1, dtype=jnp.int32)[None, :]
    edge = (length - counts)[:, None]
    keep = jnp.any(here & (places > edge), axis=0)
    at = jnp.any(here & (places == edge), axis=0)
    half = jnp.arange(length // 2, dtype=jnp.int32)[None, :]
    ok = jnp.any(here & (half >= length // 2 - (counts // 2)[:, None]), axis=0)
    return keep, at, ok


def taps(padded, axes, halves):
    pieces = []
    for off_x in range(3):
        for off_y in range(3):
            for off_z in range(3):
                piece = padded
                for axis_no, offset, half in zip(axes, (off_x, off_y, off_z), halves):
                    piece = lax.slice_in_dim(piece, offset, offset + 2 * half - 1, 2, axis_no)
                pieces.append(piece)
    return pieces


def local(fields, rows_live, cols_live, weight, bias, grad_out):
    in_chans, cap_x, cap_y, depth = fields.shape
    half_x = cap_x // 2
    half_y = cap_y // 2
    half_z = depth // 2
    out_chans = weight.shape[0]
    tiles_y = lax.axis_size("gy")
    cell_grad = lax.all_to_all(grad_out, "gy", split_axis=2, concat_axis=0, tiled=True)
    row_keep, row_at, row_ok = count_masks(rows_live, "gx", cap_x)
    col_keep, col_at, col_ok = count_masks(cols_live, "gy", cap_y)
    above = from_behind(fields[:, cap_x - 1], "gx", 1)
    ext_rows = extend(fields, above, row_keep, row_at, 1)
    beside = from_behind(ext_rows[:, :, cap_y - 1], "gy", 1)
    ext_full = extend(ext_rows, beside, col_keep, col_at, 2)
    lanes = jnp.arange(3 * half_z, dtype=jnp.int32)
    source = 2 * (lanes % half_z) + lanes // half_z - 1
    pick = (jnp.arange(depth, dtype=jnp.int32)[:, None] == source[None, :]).astype(fields.dtype)
    ztaps = jnp.einsum("cxyz,zk->cxyk", ext_full, pick, preferred_element_type=jnp.float32)
    ztaps = ztaps.astype(fields.dtype)
    rows = jnp.arange(3 * half_y, dtype=jnp.int32)
    row_source = 2 * (rows % half_y) + rows // half_y
    row_pick = (row_source[:, None] == jnp.arange(cap_y + 1, dtype=jnp.int32)[None, :]).astype(fields.dtype)
    row_pick = jnp.broadcast_to(row_pick, (in_chans, cap_x + 1) + row_pick.shape)
    yztaps = jnp.einsum("cxjy,cxyk->cxjk", row_pick, ztaps, preferred_element_type=jnp.float32)
    yztaps = yztaps.astype(fields.dtype)
    blocks = []
    for off_x in range(3):
        for off_y in range(3):
            blocks.append(yztaps[:, off_x : off_x + 2 * half_x - 1 : 2, off_y * half_y : (off_y + 1) * half_y])
    stacked = jnp.stack(blocks, axis=1).reshape(in_chans * 9, half_x, half_y, 3 * half_z)
    kernel = weight.reshape(out_chans, in_chans * 9, 3)
    conv = bias[:, None, None, None]
    for off_z in range(3):
        part = stacked[..., off_z * half_z : (off_z + 1) * half_z]
        conv = conv + jnp.einsum("ok,kpqr->opqr", kernel[:, :, off_z], part, preferred_element_type=jnp.float32)
    live = (row_ok[:, None] & col_ok[None, :]).reshape(1, half_x, half_y, 1)
    pre_wide = lax.reduce_precision(jnp.where(live, conv, 0.0), exponent_bits=8, mantissa_bits=7)
    sigma = jax.nn.sigmoid(pre_wide)
    stem_local = (pre_wide * sigma).astype(jnp.bfloat16)
    slope = sigma * (1.0 + pre_wide * (1.0 - sigma))
    grad_wide = jnp.where(live, cell_grad.astype(jnp.float32) * slope, 0.0)
    grad_wide = lax.reduce_precision(grad_wide, exponent_bits=8, mantissa_bits=7)
    returned = grad_wide.astype(jnp.bfloat16)
    stem = lax.all_to_all(stem_local, "gy", split_axis=0, concat_axis=2, tiled=True)
    grads = []
    for off_z in range(3):
        part = stacked[..., off_z * half_z : (off_z + 1) * half_z]
        grads.append(jnp.einsum("opqr,kpqr->ok", returned, part, preferred_element_type=jnp.float32))
    weight_full = jnp.stack(grads, axis=-1).reshape(out_chans, -1)
    bias_full = jnp.sum(grad_wide, axis=(1, 2, 3))
    packed = jnp.concatenate([weight_full, bias_full[:, None]], axis=1)
    total = butterfly_sum(butterfly_sum(packed, "gx"), "gy")
    share = out_chans // tiles_y
    mine = lax.dynamic_slice_in_dim(total, lax.axis_index("gy") * share, share, 0)
    weight_grad, bias_grad = mine[:, :-1], mine[:, -1]
    return (stem, weight_grad, bias_grad)


def solution(mesh):
    in_specs = (P(None, "gx", "gy", None), P(), P(), P(), P(), P("gy", "gx", None, None))
    out_specs = (P("gy", "gx", None, None), P("gy", None), P("gy"))
    return jax.shard_map(local, mesh=mesh, in_specs=in_specs, out_specs=out_specs, check_vma=False)
```

```python
import jax
import jax.numpy as jnp
from jax import lax
from jax.sharding import PartitionSpec as P


def from_behind(block, axis, distance):
    devices = range(lax.axis_size(axis))
    route = [(i - distance, i) for i in devices if i - distance in devices]
    return lax.ppermute(block, axis, route)


def butterfly_sum(value, axis):
    size = lax.axis_size(axis)
    if size & (size - 1):
        return lax.psum(value, axis)
    step = 1
    while step < size:
        swap = [(i, i ^ step) for i in range(size)]
        value = value + lax.ppermute(value, axis, swap)
        step *= 2
    return value


def extend(data, border, keep, at, dim):
    length = data.shape[dim]
    border_wide = jnp.expand_dims(border, dim)
    joined = jnp.concatenate([jnp.zeros_like(border_wide), data], axis=dim)
    shape = [1] * joined.ndim
    shape[dim] = length + 1
    kept = jnp.where(keep.reshape(shape), joined, jnp.zeros_like(joined))
    return jnp.where(at.reshape(shape), border_wide, kept)


def count_masks(counts, axis, length):
    here = (jnp.arange(counts.shape[0], dtype=jnp.int32) == lax.axis_index(axis))[:, None]
    places = jnp.arange(length + 1, dtype=jnp.int32)[None, :]
    edge = (length - counts)[:, None]
    keep = jnp.any(here & (places > edge), axis=0)
    at = jnp.any(here & (places == edge), axis=0)
    half = jnp.arange(length // 2, dtype=jnp.int32)[None, :]
    ok = jnp.any(here & (half >= length // 2 - (counts // 2)[:, None]), axis=0)
    return keep, at, ok


def taps(padded, axes, halves):
    pieces = []
    for off_x in range(3):
        for off_y in range(3):
            for off_z in range(3):
                piece = padded
                for axis_no, offset, half in zip(axes, (off_x, off_y, off_z), halves):
                    piece = lax.slice_in_dim(piece, offset, offset + 2 * half - 1, 2, axis_no)
                pieces.append(piece)
    return pieces


def local(fields, rows_live, cols_live, weight, bias, grad_out):
    in_chans, cap_x, cap_y, depth = fields.shape
    half_x = cap_x // 2
    half_y = cap_y // 2
    half_z = depth // 2
    out_chans = weight.shape[0]
    tiles_y = lax.axis_size("gy")
    chans, rows_x, cols_all, lanes_z = grad_out.shape
    out_parts = grad_out.reshape(chans, rows_x, tiles_y, cols_all // tiles_y, lanes_z).transpose(2, 0, 1, 3, 4)
    out_parts = out_parts.reshape(tiles_y, chans * rows_x, cols_all // tiles_y, lanes_z)
    cell_grad = lax.all_to_all(out_parts, "gy", split_axis=0, concat_axis=0, tiled=True)
    cell_grad = cell_grad.reshape(tiles_y * chans, rows_x, cols_all // tiles_y, lanes_z)
    row_keep, row_at, row_ok = count_masks(rows_live, "gx", cap_x)
    col_keep, col_at, col_ok = count_masks(cols_live, "gy", cap_y)
    above = from_behind(fields[:, cap_x - 1], "gx", 1)
    ext_rows = extend(fields, above, row_keep, row_at, 1)
    beside = from_behind(ext_rows[:, :, cap_y - 1], "gy", 1)
    ext_full = extend(ext_rows, beside, col_keep, col_at, 2)
    lanes = jnp.arange(3 * half_z, dtype=jnp.int32)
    source = 2 * (lanes % half_z) + lanes // half_z - 1
    pick = (jnp.arange(depth, dtype=jnp.int32)[:, None] == source[None, :]).astype(fields.dtype)
    ztaps = jnp.einsum("cxyz,zk->cxyk", ext_full, pick, preferred_element_type=jnp.float32)
    ztaps = ztaps.astype(fields.dtype)
    rows = jnp.arange(3 * half_y, dtype=jnp.int32)
    row_source = 2 * (rows % half_y) + rows // half_y
    row_pick = (row_source[:, None] == jnp.arange(cap_y + 1, dtype=jnp.int32)[None, :]).astype(fields.dtype)
    row_pick = jnp.broadcast_to(row_pick, (in_chans, cap_x + 1) + row_pick.shape)
    yztaps = jnp.einsum("cxjy,cxyk->cxjk", row_pick, ztaps, preferred_element_type=jnp.float32)
    yztaps = yztaps.astype(fields.dtype)
    blocks = []
    for off_x in range(3):
        for off_y in range(3):
            blocks.append(yztaps[:, off_x : off_x + 2 * half_x - 1 : 2, off_y * half_y : (off_y + 1) * half_y])
    stacked = jnp.stack(blocks, axis=1).reshape(in_chans * 9, half_x, half_y, 3 * half_z)
    kernel = weight.reshape(out_chans, in_chans * 9, 3)
    conv = bias[:, None, None, None]
    for off_z in range(3):
        part = stacked[..., off_z * half_z : (off_z + 1) * half_z]
        conv = conv + jnp.einsum("ok,kpqr->opqr", kernel[:, :, off_z], part, preferred_element_type=jnp.float32)
    live = (row_ok[:, None] & col_ok[None, :]).reshape(1, half_x, half_y, 1)
    pre_wide = lax.reduce_precision(jnp.where(live, conv, 0.0), exponent_bits=8, mantissa_bits=7)
    sigma = jax.nn.sigmoid(pre_wide)
    stem_local = (pre_wide * sigma).astype(jnp.bfloat16)
    slope = sigma * (1.0 + pre_wide * (1.0 - sigma))
    grad_wide = jnp.where(live, cell_grad.astype(jnp.float32) * slope, 0.0)
    grad_wide = lax.reduce_precision(grad_wide, exponent_bits=8, mantissa_bits=7)
    returned = grad_wide.astype(jnp.bfloat16)
    stem_parts = stem_local.reshape(tiles_y, chans * rows_x, cols_all // tiles_y, lanes_z)
    stem = lax.all_to_all(stem_parts, "gy", split_axis=0, concat_axis=0, tiled=True)
    stem = stem.reshape(tiles_y, chans, rows_x, cols_all // tiles_y, lanes_z)
    stem = stem.transpose(1, 2, 0, 3, 4).reshape(chans, rows_x, cols_all, lanes_z)
    grads = []
    for off_z in range(3):
        part = stacked[..., off_z * half_z : (off_z + 1) * half_z]
        grads.append(jnp.einsum("opqr,kpqr->ok", returned, part, preferred_element_type=jnp.float32))
    weight_full = jnp.stack(grads, axis=-1).reshape(out_chans, -1)
    bias_full = jnp.sum(grad_wide, axis=(1, 2, 3))
    packed = jnp.concatenate([weight_full, bias_full[:, None]], axis=1)
    total = butterfly_sum(butterfly_sum(packed, "gx"), "gy")
    share = out_chans // tiles_y
    mine = lax.dynamic_slice_in_dim(total, lax.axis_index("gy") * share, share, 0)
    weight_grad, bias_grad = mine[:, :-1], mine[:, -1]
    return (stem, weight_grad, bias_grad)


def solution(mesh):
    in_specs = (P(None, "gx", "gy", None), P(), P(), P(), P(), P("gy", "gx", None, None))
    out_specs = (P("gy", "gx", None, None), P("gy", None), P("gy"))
    return jax.shard_map(local, mesh=mesh, in_specs=in_specs, out_specs=out_specs, check_vma=False)
```

```python
import jax
import jax.numpy as jnp
from jax import lax
from jax.sharding import PartitionSpec as P


def from_behind(block, axis, distance):
    devices = range(lax.axis_size(axis))
    route = [(i - distance, i) for i in devices if i - distance in devices]
    return lax.ppermute(block, axis, route)


def butterfly_sum(value, axis):
    size = lax.axis_size(axis)
    if size & (size - 1):
        return lax.psum(value, axis)
    step = size // 2
    while step:
        swap = [(i, i ^ step) for i in range(size)]
        value = value + lax.ppermute(value, axis, swap)
        step //= 2
    return value


def extend(data, border, keep, at, dim):
    length = data.shape[dim]
    border_wide = jnp.expand_dims(border, dim)
    joined = jnp.concatenate([jnp.zeros_like(border_wide), data], axis=dim)
    shape = [1] * joined.ndim
    shape[dim] = length + 1
    kept = jnp.where(keep.reshape(shape), joined, jnp.zeros_like(joined))
    return jnp.where(at.reshape(shape), border_wide, kept)


def count_masks(counts, axis, length):
    here = (jnp.arange(counts.shape[0], dtype=jnp.int32) == lax.axis_index(axis))[:, None]
    places = jnp.arange(length + 1, dtype=jnp.int32)[None, :]
    edge = (length - counts)[:, None]
    keep = jnp.any(here & (places > edge), axis=0)
    at = jnp.any(here & (places == edge), axis=0)
    half = jnp.arange(length // 2, dtype=jnp.int32)[None, :]
    ok = jnp.any(here & (half >= length // 2 - (counts // 2)[:, None]), axis=0)
    return keep, at, ok


def taps(padded, axes, halves):
    pieces = []
    for off_x in range(3):
        for off_y in range(3):
            for off_z in range(3):
                piece = padded
                for axis_no, offset, half in zip(axes, (off_x, off_y, off_z), halves):
                    piece = lax.slice_in_dim(piece, offset, offset + 2 * half - 1, 2, axis_no)
                pieces.append(piece)
    return pieces


def local(fields, rows_live, cols_live, weight, bias, grad_out):
    in_chans, cap_x, cap_y, depth = fields.shape
    half_x = cap_x // 2
    half_y = cap_y // 2
    half_z = depth // 2
    out_chans = weight.shape[0]
    tiles_y = lax.axis_size("gy")
    chans, rows_x, cols_all, lanes_z = grad_out.shape
    out_parts = grad_out.reshape(chans, rows_x, tiles_y, cols_all // tiles_y, lanes_z).transpose(2, 0, 1, 3, 4)
    out_parts = out_parts.reshape(tiles_y, chans * rows_x, cols_all // tiles_y, lanes_z)
    cell_grad = lax.all_to_all(out_parts, "gy", split_axis=0, concat_axis=0, tiled=True)
    cell_grad = cell_grad.reshape(tiles_y * chans, rows_x, cols_all // tiles_y, lanes_z)
    row_keep, row_at, row_ok = count_masks(rows_live, "gx", cap_x)
    col_keep, col_at, col_ok = count_masks(cols_live, "gy", cap_y)
    above = from_behind(fields[:, cap_x - 1], "gx", 1)
    ext_rows = extend(fields, above, row_keep, row_at, 1)
    beside = from_behind(ext_rows[:, :, cap_y - 1], "gy", 1)
    ext_full = extend(ext_rows, beside, col_keep, col_at, 2)
    lanes = jnp.arange(3 * half_z, dtype=jnp.int32)
    source = 2 * (lanes % half_z) + lanes // half_z - 1
    pick = (jnp.arange(depth, dtype=jnp.int32)[:, None] == source[None, :]).astype(fields.dtype)
    ztaps = jnp.einsum("cxyz,zk->cxyk", ext_full, pick, preferred_element_type=jnp.float32)
    ztaps = ztaps.astype(fields.dtype)
    rows = jnp.arange(3 * half_y, dtype=jnp.int32)
    row_source = 2 * (rows % half_y) + rows // half_y
    row_pick = (row_source[:, None] == jnp.arange(cap_y + 1, dtype=jnp.int32)[None, :]).astype(fields.dtype)
    row_pick = jnp.broadcast_to(row_pick, (in_chans, cap_x + 1) + row_pick.shape)
    yztaps = jnp.einsum("cxjy,cxyk->cxjk", row_pick, ztaps, preferred_element_type=jnp.float32)
    yztaps = yztaps.astype(fields.dtype)
    blocks = []
    for off_x in range(3):
        for off_y in range(3):
            blocks.append(yztaps[:, off_x : off_x + 2 * half_x - 1 : 2, off_y * half_y : (off_y + 1) * half_y])
    stacked = jnp.stack(blocks, axis=1).reshape(in_chans * 9, half_x, half_y, 3 * half_z)
    kernel = weight.reshape(out_chans, in_chans * 9, 3)
    conv = bias[:, None, None, None]
    for off_z in range(3):
        part = stacked[..., off_z * half_z : (off_z + 1) * half_z]
        conv = conv + jnp.einsum("ok,kpqr->opqr", kernel[:, :, off_z], part, preferred_element_type=jnp.float32)
    live = (row_ok[:, None] & col_ok[None, :]).reshape(1, half_x, half_y, 1)
    pre_wide = lax.reduce_precision(jnp.where(live, conv, 0.0), exponent_bits=8, mantissa_bits=7)
    sigma = jax.nn.sigmoid(pre_wide)
    stem_local = (pre_wide * sigma).astype(jnp.bfloat16)
    slope = sigma * (1.0 + pre_wide * (1.0 - sigma))
    grad_wide = jnp.where(live, cell_grad.astype(jnp.float32) * slope, 0.0)
    grad_wide = lax.reduce_precision(grad_wide, exponent_bits=8, mantissa_bits=7)
    returned = grad_wide.astype(jnp.bfloat16)
    stem_parts = stem_local.reshape(tiles_y, chans * rows_x, cols_all // tiles_y, lanes_z)
    stem = lax.all_to_all(stem_parts, "gy", split_axis=0, concat_axis=0, tiled=True)
    stem = stem.reshape(tiles_y, chans, rows_x, cols_all // tiles_y, lanes_z)
    stem = stem.transpose(1, 2, 0, 3, 4).reshape(chans, rows_x, cols_all, lanes_z)
    grads = []
    for off_z in range(3):
        part = stacked[..., off_z * half_z : (off_z + 1) * half_z]
        grads.append(jnp.einsum("opqr,kpqr->ok", returned, part, preferred_element_type=jnp.float32))
    weight_full = jnp.stack(grads, axis=-1).reshape(out_chans, -1)
    bias_full = jnp.sum(grad_wide, axis=(1, 2, 3))
    packed = jnp.concatenate([weight_full, bias_full[:, None]], axis=1)
    total = butterfly_sum(butterfly_sum(packed, "gx"), "gy")
    share = out_chans // tiles_y
    mine = lax.dynamic_slice_in_dim(total, lax.axis_index("gy") * share, share, 0)
    weight_grad, bias_grad = mine[:, :-1], mine[:, -1]
    return (stem, weight_grad, bias_grad)


def solution(mesh):
    in_specs = (P(None, "gx", "gy", None), P(), P(), P(), P(), P("gy", "gx", None, None))
    out_specs = (P("gy", "gx", None, None), P("gy", None), P("gy"))
    return jax.shard_map(local, mesh=mesh, in_specs=in_specs, out_specs=out_specs, check_vma=False)
```

```python
import jax
import jax.numpy as jnp
from jax import lax
from jax.sharding import PartitionSpec as P


def from_behind(block, axis, distance):
    devices = range(lax.axis_size(axis))
    route = [(i - distance, i) for i in devices if i - distance in devices]
    return lax.ppermute(block, axis, route)


def butterfly_sum(value, axis):
    size = lax.axis_size(axis)
    if size & (size - 1):
        return lax.psum(value, axis)
    step = size // 2
    while step:
        swap = [(i, i ^ step) for i in range(size)]
        value = value + lax.ppermute(value, axis, swap)
        step //= 2
    return value


def extend(data, border, keep, at, dim):
    length = data.shape[dim]
    border_wide = jnp.expand_dims(border, dim)
    joined = jnp.concatenate([jnp.zeros_like(border_wide), data], axis=dim)
    shape = [1] * joined.ndim
    shape[dim] = length + 1
    kept = jnp.where(keep.reshape(shape), joined, jnp.zeros_like(joined))
    return jnp.where(at.reshape(shape), border_wide, kept)


def count_masks(counts, axis, length):
    here = (jnp.arange(counts.shape[0], dtype=jnp.int32) == lax.axis_index(axis))[:, None]
    places = jnp.arange(length + 1, dtype=jnp.int32)[None, :]
    edge = (length - counts)[:, None]
    keep = jnp.any(here & (places > edge), axis=0)
    at = jnp.any(here & (places == edge), axis=0)
    half = jnp.arange(length // 2, dtype=jnp.int32)[None, :]
    ok = jnp.any(here & (half >= length // 2 - (counts // 2)[:, None]), axis=0)
    return keep, at, ok


def taps(padded, axes, halves):
    pieces = []
    for off_x in range(3):
        for off_y in range(3):
            for off_z in range(3):
                piece = padded
                for axis_no, offset, half in zip(axes, (off_x, off_y, off_z), halves):
                    piece = lax.slice_in_dim(piece, offset, offset + 2 * half - 1, 2, axis_no)
                pieces.append(piece)
    return pieces


def local(fields, rows_live, cols_live, weight, bias, grad_out):
    in_chans, cap_x, cap_y, depth = fields.shape
    half_x = cap_x // 2
    half_y = cap_y // 2
    half_z = depth // 2
    out_chans = weight.shape[0]
    tiles_y = lax.axis_size("gy")
    chans, rows_x, cols_all, lanes_z = grad_out.shape
    out_parts = grad_out.reshape(chans, rows_x, tiles_y, cols_all // tiles_y, lanes_z).transpose(2, 0, 1, 3, 4)
    out_parts = out_parts.reshape(tiles_y, chans * rows_x, cols_all // tiles_y, lanes_z)
    cell_grad = lax.all_to_all(out_parts, "gy", split_axis=0, concat_axis=0, tiled=True)
    cell_grad = cell_grad.reshape(tiles_y * chans, rows_x, cols_all // tiles_y, lanes_z)
    row_keep, row_at, row_ok = count_masks(rows_live, "gx", cap_x)
    col_keep, col_at, col_ok = count_masks(cols_live, "gy", cap_y)
    above = from_behind(fields[:, cap_x - 1], "gx", 1)
    ext_rows = extend(fields, above, row_keep, row_at, 1)
    beside = from_behind(ext_rows[:, :, cap_y - 1], "gy", 1)
    ext_full = extend(ext_rows, beside, col_keep, col_at, 2)
    lanes = jnp.arange(3 * half_z, dtype=jnp.int32)
    source = 2 * (lanes % half_z) + lanes // half_z - 1
    pick = (jnp.arange(depth, dtype=jnp.int32)[:, None] == source[None, :]).astype(fields.dtype)
    ztaps = jnp.einsum("cxyz,zk->cxyk", ext_full, pick, preferred_element_type=jnp.float32)
    ztaps = ztaps.astype(fields.dtype)
    rows = jnp.arange(3 * half_y, dtype=jnp.int32)
    row_source = 2 * (rows % half_y) + rows // half_y
    row_pick = (row_source[:, None] == jnp.arange(cap_y + 1, dtype=jnp.int32)[None, :]).astype(fields.dtype)
    row_pick = jnp.broadcast_to(row_pick, (in_chans, cap_x + 1) + row_pick.shape)
    yztaps = jnp.einsum("cxjy,cxyk->cxjk", row_pick, ztaps, preferred_element_type=jnp.float32)
    yztaps = yztaps.astype(fields.dtype)
    blocks = []
    for off_x in range(3):
        for off_y in range(3):
            blocks.append(yztaps[:, off_x : off_x + 2 * half_x - 1 : 2, off_y * half_y : (off_y + 1) * half_y])
    stacked = jnp.stack(blocks, axis=1).reshape(in_chans * 9, half_x, half_y, 3 * half_z)
    kernel = weight.reshape(out_chans, in_chans * 9, 3)
    conv = bias[:, None, None, None]
    for off_z in range(3):
        part = stacked[..., off_z * half_z : (off_z + 1) * half_z]
        conv = conv + jnp.einsum("ok,kpqr->opqr", kernel[:, :, off_z], part, preferred_element_type=jnp.float32)
    live = (row_ok[:, None] & col_ok[None, :]).reshape(1, half_x, half_y, 1)
    pre_wide = lax.reduce_precision(jnp.where(live, conv, 0.0), exponent_bits=8, mantissa_bits=7)
    sigma = jax.nn.sigmoid(pre_wide)
    stem_local = (pre_wide * sigma).astype(jnp.bfloat16)
    slope = sigma * (1.0 + pre_wide * (1.0 - sigma))
    grad_wide = jnp.where(live, cell_grad.astype(jnp.float32) * slope, 0.0)
    grad_wide = lax.reduce_precision(grad_wide, exponent_bits=8, mantissa_bits=7)
    returned = grad_wide.astype(jnp.bfloat16)
    grads = []
    for off_z in range(3):
        part = stacked[..., off_z * half_z : (off_z + 1) * half_z]
        grads.append(jnp.einsum("opqr,kpqr->ok", returned, part, preferred_element_type=jnp.float32))
    weight_full = jnp.stack(grads, axis=-1).reshape(out_chans, -1)
    bias_full = jnp.sum(grad_wide, axis=(1, 2, 3))
    packed = jnp.concatenate([weight_full, bias_full[:, None]], axis=1)
    share = out_chans // tiles_y
    high = packed.astype(jnp.bfloat16)
    low = (packed - high.astype(jnp.float32)).astype(jnp.bfloat16)
    coded = jnp.stack([high, low]).reshape(2, tiles_y, -1).transpose(1, 0, 2).reshape(tiles_y, -1)
    tile = (cols_all // tiles_y) * lanes_z
    extra = -(-coded.shape[1] // tile)
    coded = jnp.pad(coded, ((0, 0), (0, extra * tile - coded.shape[1])))
    coded = coded.reshape(tiles_y, extra, cols_all // tiles_y, lanes_z)
    stem_parts = stem_local.reshape(tiles_y, chans * rows_x, cols_all // tiles_y, lanes_z)
    sent = jnp.concatenate([stem_parts, coded], axis=1)
    got = lax.all_to_all(sent, "gy", split_axis=0, concat_axis=0, tiled=True)
    stem = got[:, : chans * rows_x].reshape(tiles_y, chans, rows_x, cols_all // tiles_y, lanes_z)
    stem = stem.transpose(1, 2, 0, 3, 4).reshape(chans, rows_x, cols_all, lanes_z)
    width = packed.shape[1]
    pieces = got[:, chans * rows_x :].reshape(tiles_y, -1)[:, : 2 * share * width]
    pieces = pieces.reshape(tiles_y, 2, share, width).astype(jnp.float32)
    part = jnp.sum(pieces[:, 0] + pieces[:, 1], axis=0)
    total = butterfly_sum(part, "gx")
    weight_grad, bias_grad = total[:, :-1], total[:, -1]
    return (stem, weight_grad, bias_grad)


def solution(mesh):
    in_specs = (P(None, "gx", "gy", None), P(), P(), P(), P(), P("gy", "gx", None, None))
    out_specs = (P("gy", "gx", None, None), P("gy", None), P("gy"))
    return jax.shard_map(local, mesh=mesh, in_specs=in_specs, out_specs=out_specs, check_vma=False)
```

```python
import jax
import jax.numpy as jnp
from jax import lax
from jax.sharding import PartitionSpec as P


def from_behind(block, axis, distance):
    devices = range(lax.axis_size(axis))
    route = [(i - distance, i) for i in devices if i - distance in devices]
    return lax.ppermute(block, axis, route)


def butterfly_sum(value, axis):
    size = lax.axis_size(axis)
    if size & (size - 1):
        return lax.psum(value, axis)
    bits = size.bit_length() - 1
    while bits:
        low = max(bits - 2, 0)
        spans = [(1 << low) * t for t in range(1, 1 << (bits - low))]
        got = [lax.ppermute(value, axis, [(i, i ^ t) for i in range(size)]) for t in spans]
        if len(got) == 1:
            value = value + got[0]
        else:
            value = (value + got[0]) + (got[1] + got[2])
        bits = low
    return value


def extend(data, border, keep, at, dim):
    length = data.shape[dim]
    border_wide = jnp.expand_dims(border, dim)
    joined = jnp.concatenate([jnp.zeros_like(border_wide), data], axis=dim)
    shape = [1] * joined.ndim
    shape[dim] = length + 1
    kept = jnp.where(keep.reshape(shape), joined, jnp.zeros_like(joined))
    return jnp.where(at.reshape(shape), border_wide, kept)


def count_masks(counts, axis, length):
    here = (jnp.arange(counts.shape[0], dtype=jnp.int32) == lax.axis_index(axis))[:, None]
    places = jnp.arange(length + 1, dtype=jnp.int32)[None, :]
    edge = (length - counts)[:, None]
    keep = jnp.any(here & (places > edge), axis=0)
    at = jnp.any(here & (places == edge), axis=0)
    half = jnp.arange(length // 2, dtype=jnp.int32)[None, :]
    ok = jnp.any(here & (half >= length // 2 - (counts // 2)[:, None]), axis=0)
    return keep, at, ok


def taps(padded, axes, halves):
    pieces = []
    for off_x in range(3):
        for off_y in range(3):
            for off_z in range(3):
                piece = padded
                for axis_no, offset, half in zip(axes, (off_x, off_y, off_z), halves):
                    piece = lax.slice_in_dim(piece, offset, offset + 2 * half - 1, 2, axis_no)
                pieces.append(piece)
    return pieces


def local(fields, rows_live, cols_live, weight, bias, grad_out):
    in_chans, cap_x, cap_y, depth = fields.shape
    half_x = cap_x // 2
    half_y = cap_y // 2
    half_z = depth // 2
    out_chans = weight.shape[0]
    tiles_y = lax.axis_size("gy")
    cell_grad = lax.all_to_all(grad_out, "gy", split_axis=2, concat_axis=0, tiled=True)
    row_keep, row_at, row_ok = count_masks(rows_live, "gx", cap_x)
    col_keep, col_at, col_ok = count_masks(cols_live, "gy", cap_y)
    above = from_behind(fields[:, cap_x - 1], "gx", 1)
    ext_rows = extend(fields, above, row_keep, row_at, 1)
    beside = from_behind(ext_rows[:, :, cap_y - 1], "gy", 1)
    ext_full = extend(ext_rows, beside, col_keep, col_at, 2)
    lanes = jnp.arange(3 * half_z, dtype=jnp.int32)
    source = 2 * (lanes % half_z) + lanes // half_z - 1
    pick = (jnp.arange(depth, dtype=jnp.int32)[:, None] == source[None, :]).astype(fields.dtype)
    ztaps = jnp.einsum("cxyz,zk->cxyk", ext_full, pick, preferred_element_type=jnp.float32)
    ztaps = ztaps.astype(fields.dtype)
    rows = jnp.arange(3 * half_y, dtype=jnp.int32)
    row_source = 2 * (rows % half_y) + rows // half_y
    row_pick = (row_source[:, None] == jnp.arange(cap_y + 1, dtype=jnp.int32)[None, :]).astype(fields.dtype)
    row_pick = jnp.broadcast_to(row_pick, (in_chans, cap_x + 1) + row_pick.shape)
    yztaps = jnp.einsum("cxjy,cxyk->cxjk", row_pick, ztaps, preferred_element_type=jnp.float32)
    yztaps = yztaps.astype(fields.dtype)
    blocks = []
    for off_x in range(3):
        for off_y in range(3):
            blocks.append(yztaps[:, off_x : off_x + 2 * half_x - 1 : 2, off_y * half_y : (off_y + 1) * half_y])
    stacked = jnp.stack(blocks, axis=1).reshape(in_chans * 9, half_x, half_y, 3 * half_z)
    kernel = weight.reshape(out_chans, in_chans * 9, 3)
    conv = bias[:, None, None, None]
    for off_z in range(3):
        part = stacked[..., off_z * half_z : (off_z + 1) * half_z]
        conv = conv + jnp.einsum("ok,kpqr->opqr", kernel[:, :, off_z], part, preferred_element_type=jnp.float32)
    live = (row_ok[:, None] & col_ok[None, :]).reshape(1, half_x, half_y, 1)
    pre_wide = lax.reduce_precision(jnp.where(live, conv, 0.0), exponent_bits=8, mantissa_bits=7)
    sigma = jax.nn.sigmoid(pre_wide)
    stem_local = (pre_wide * sigma).astype(jnp.bfloat16)
    slope = sigma * (1.0 + pre_wide * (1.0 - sigma))
    grad_wide = jnp.where(live, cell_grad.astype(jnp.float32) * slope, 0.0)
    grad_wide = lax.reduce_precision(grad_wide, exponent_bits=8, mantissa_bits=7)
    returned = grad_wide.astype(jnp.bfloat16)
    stem = lax.all_to_all(stem_local, "gy", split_axis=0, concat_axis=2, tiled=True)
    grads = []
    for off_z in range(3):
        part = stacked[..., off_z * half_z : (off_z + 1) * half_z]
        grads.append(jnp.einsum("opqr,kpqr->ok", returned, part, preferred_element_type=jnp.float32))
    weight_full = jnp.stack(grads, axis=-1).reshape(out_chans, -1)
    bias_full = jnp.sum(grad_wide, axis=(1, 2, 3))
    packed = jnp.concatenate([weight_full, bias_full[:, None]], axis=1)
    total = butterfly_sum(butterfly_sum(packed, "gx"), "gy")
    share = out_chans // tiles_y
    mine = lax.dynamic_slice_in_dim(total, lax.axis_index("gy") * share, share, 0)
    weight_grad, bias_grad = mine[:, :-1], mine[:, -1]
    return (stem, weight_grad, bias_grad)


def solution(mesh):
    in_specs = (P(None, "gx", "gy", None), P(), P(), P(), P(), P("gy", "gx", None, None))
    out_specs = (P("gy", "gx", None, None), P("gy", None), P("gy"))
    return jax.shard_map(local, mesh=mesh, in_specs=in_specs, out_specs=out_specs, check_vma=False)
```

```python
import jax
import jax.numpy as jnp
from jax import lax
from jax.sharding import PartitionSpec as P


def from_behind(block, axis, distance):
    devices = range(lax.axis_size(axis))
    route = [(i - distance, i) for i in devices if i - distance in devices]
    return lax.ppermute(block, axis, route)


def butterfly_sum(value, axis):
    size = lax.axis_size(axis)
    if size & (size - 1):
        return lax.psum(value, axis)
    bits = size.bit_length() - 1
    while bits:
        low = max(bits - 3, 0)
        spans = [(1 << low) * t for t in range(1, 1 << (bits - low))]
        vals = [value] + [lax.ppermute(value, axis, [(i, i ^ t) for i in range(size)]) for t in spans]
        while len(vals) > 1:
            vals = [vals[k] + vals[k + 1] for k in range(0, len(vals), 2)]
        value = vals[0]
        bits = low
    return value


def extend(data, border, keep, at, dim):
    length = data.shape[dim]
    border_wide = jnp.expand_dims(border, dim)
    joined = jnp.concatenate([jnp.zeros_like(border_wide), data], axis=dim)
    shape = [1] * joined.ndim
    shape[dim] = length + 1
    kept = jnp.where(keep.reshape(shape), joined, jnp.zeros_like(joined))
    return jnp.where(at.reshape(shape), border_wide, kept)


def count_masks(counts, axis, length):
    here = (jnp.arange(counts.shape[0], dtype=jnp.int32) == lax.axis_index(axis))[:, None]
    places = jnp.arange(length + 1, dtype=jnp.int32)[None, :]
    edge = (length - counts)[:, None]
    keep = jnp.any(here & (places > edge), axis=0)
    at = jnp.any(here & (places == edge), axis=0)
    half = jnp.arange(length // 2, dtype=jnp.int32)[None, :]
    ok = jnp.any(here & (half >= length // 2 - (counts // 2)[:, None]), axis=0)
    return keep, at, ok


def taps(padded, axes, halves):
    pieces = []
    for off_x in range(3):
        for off_y in range(3):
            for off_z in range(3):
                piece = padded
                for axis_no, offset, half in zip(axes, (off_x, off_y, off_z), halves):
                    piece = lax.slice_in_dim(piece, offset, offset + 2 * half - 1, 2, axis_no)
                pieces.append(piece)
    return pieces


def local(fields, rows_live, cols_live, weight, bias, grad_out):
    in_chans, cap_x, cap_y, depth = fields.shape
    half_x = cap_x // 2
    half_y = cap_y // 2
    half_z = depth // 2
    out_chans = weight.shape[0]
    tiles_y = lax.axis_size("gy")
    cell_grad = lax.all_to_all(grad_out, "gy", split_axis=2, concat_axis=0, tiled=True)
    row_keep, row_at, row_ok = count_masks(rows_live, "gx", cap_x)
    col_keep, col_at, col_ok = count_masks(cols_live, "gy", cap_y)
    above = from_behind(fields[:, cap_x - 1], "gx", 1)
    ext_rows = extend(fields, above, row_keep, row_at, 1)
    beside = from_behind(ext_rows[:, :, cap_y - 1], "gy", 1)
    ext_full = extend(ext_rows, beside, col_keep, col_at, 2)
    lanes = jnp.arange(3 * half_z, dtype=jnp.int32)
    source = 2 * (lanes % half_z) + lanes // half_z - 1
    pick = (jnp.arange(depth, dtype=jnp.int32)[:, None] == source[None, :]).astype(fields.dtype)
    ztaps = jnp.einsum("cxyz,zk->cxyk", ext_full, pick, preferred_element_type=jnp.float32)
    ztaps = ztaps.astype(fields.dtype)
    rows = jnp.arange(3 * half_y, dtype=jnp.int32)
    row_source = 2 * (rows % half_y) + rows // half_y
    row_pick = (row_source[:, None] == jnp.arange(cap_y + 1, dtype=jnp.int32)[None, :]).astype(fields.dtype)
    row_pick = jnp.broadcast_to(row_pick, (in_chans, cap_x + 1) + row_pick.shape)
    yztaps = jnp.einsum("cxjy,cxyk->cxjk", row_pick, ztaps, preferred_element_type=jnp.float32)
    yztaps = yztaps.astype(fields.dtype)
    blocks = []
    for off_x in range(3):
        for off_y in range(3):
            blocks.append(yztaps[:, off_x : off_x + 2 * half_x - 1 : 2, off_y * half_y : (off_y + 1) * half_y])
    stacked = jnp.stack(blocks, axis=1).reshape(in_chans * 9, half_x, half_y, 3 * half_z)
    kernel = weight.reshape(out_chans, in_chans * 9, 3)
    conv = bias[:, None, None, None]
    for off_z in range(3):
        part = stacked[..., off_z * half_z : (off_z + 1) * half_z]
        conv = conv + jnp.einsum("ok,kpqr->opqr", kernel[:, :, off_z], part, preferred_element_type=jnp.float32)
    live = (row_ok[:, None] & col_ok[None, :]).reshape(1, half_x, half_y, 1)
    pre_wide = lax.reduce_precision(jnp.where(live, conv, 0.0), exponent_bits=8, mantissa_bits=7)
    sigma = jax.nn.sigmoid(pre_wide)
    stem_local = (pre_wide * sigma).astype(jnp.bfloat16)
    slope = sigma * (1.0 + pre_wide * (1.0 - sigma))
    grad_wide = jnp.where(live, cell_grad.astype(jnp.float32) * slope, 0.0)
    grad_wide = lax.reduce_precision(grad_wide, exponent_bits=8, mantissa_bits=7)
    returned = grad_wide.astype(jnp.bfloat16)
    stem = lax.all_to_all(stem_local, "gy", split_axis=0, concat_axis=2, tiled=True)
    grads = []
    for off_z in range(3):
        part = stacked[..., off_z * half_z : (off_z + 1) * half_z]
        grads.append(jnp.einsum("opqr,kpqr->ok", returned, part, preferred_element_type=jnp.float32))
    weight_full = jnp.stack(grads, axis=-1).reshape(out_chans, -1)
    bias_full = jnp.sum(grad_wide, axis=(1, 2, 3))
    packed = jnp.concatenate([weight_full, bias_full[:, None]], axis=1)
    total = butterfly_sum(butterfly_sum(packed, "gx"), "gy")
    share = out_chans // tiles_y
    mine = lax.dynamic_slice_in_dim(total, lax.axis_index("gy") * share, share, 0)
    weight_grad, bias_grad = mine[:, :-1], mine[:, -1]
    return (stem, weight_grad, bias_grad)


def solution(mesh):
    in_specs = (P(None, "gx", "gy", None), P(), P(), P(), P(), P("gy", "gx", None, None))
    out_specs = (P("gy", "gx", None, None), P("gy", None), P("gy"))
    return jax.shard_map(local, mesh=mesh, in_specs=in_specs, out_specs=out_specs, check_vma=False)
```

```python
import jax
import jax.numpy as jnp
from jax import lax
from jax.sharding import PartitionSpec as P


def from_behind(block, axis, distance):
    devices = range(lax.axis_size(axis))
    route = [(i - distance, i) for i in devices if i - distance in devices]
    return lax.ppermute(block, axis, route)


def butterfly_sum(value, axis):
    size = lax.axis_size(axis)
    if size & (size - 1):
        return lax.psum(value, axis)
    bits = size.bit_length() - 1
    while bits:
        low = max(bits - 2, 0)
        spans = [(1 << low) * t for t in range(1, 1 << (bits - low))]
        got = [lax.ppermute(value, axis, [(i, i ^ t) for i in range(size)]) for t in spans]
        if len(got) == 1:
            value = value + got[0]
        else:
            value = (value + got[0]) + (got[1] + got[2])
        bits = low
    return value


def extend(data, border, keep, at, dim):
    length = data.shape[dim]
    border_wide = jnp.expand_dims(border, dim)
    joined = jnp.concatenate([jnp.zeros_like(border_wide), data], axis=dim)
    shape = [1] * joined.ndim
    shape[dim] = length + 1
    kept = jnp.where(keep.reshape(shape), joined, jnp.zeros_like(joined))
    return jnp.where(at.reshape(shape), border_wide, kept)


def count_masks(counts, axis, length):
    here = (jnp.arange(counts.shape[0], dtype=jnp.int32) == lax.axis_index(axis))[:, None]
    places = jnp.arange(length + 1, dtype=jnp.int32)[None, :]
    edge = (length - counts)[:, None]
    keep = jnp.any(here & (places > edge), axis=0)
    at = jnp.any(here & (places == edge), axis=0)
    half = jnp.arange(length // 2, dtype=jnp.int32)[None, :]
    ok = jnp.any(here & (half >= length // 2 - (counts // 2)[:, None]), axis=0)
    return keep, at, ok


def taps(padded, axes, halves):
    pieces = []
    for off_x in range(3):
        for off_y in range(3):
            for off_z in range(3):
                piece = padded
                for axis_no, offset, half in zip(axes, (off_x, off_y, off_z), halves):
                    piece = lax.slice_in_dim(piece, offset, offset + 2 * half - 1, 2, axis_no)
                pieces.append(piece)
    return pieces


def local(fields, rows_live, cols_live, weight, bias, grad_out):
    in_chans, cap_x, cap_y, depth = fields.shape
    half_x = cap_x // 2
    half_y = cap_y // 2
    half_z = depth // 2
    out_chans = weight.shape[0]
    tiles_y = lax.axis_size("gy")
    cell_grad = lax.all_to_all(grad_out, "gy", split_axis=2, concat_axis=0, tiled=True)
    row_keep, row_at, row_ok = count_masks(rows_live, "gx", cap_x)
    col_keep, col_at, col_ok = count_masks(cols_live, "gy", cap_y)
    above = from_behind(fields[:, cap_x - 1], "gx", 1)
    ext_rows = extend(fields, above, row_keep, row_at, 1)
    beside = from_behind(ext_rows[:, :, cap_y - 1], "gy", 1)
    ext_full = extend(ext_rows, beside, col_keep, col_at, 2)
    lanes = jnp.arange(3 * half_z, dtype=jnp.int32)
    source = 2 * (lanes % half_z) + lanes // half_z - 1
    pick = (jnp.arange(depth, dtype=jnp.int32)[:, None] == source[None, :]).astype(fields.dtype)
    ztaps = jnp.einsum("cxyz,zk->cxyk", ext_full, pick, preferred_element_type=jnp.float32)
    ztaps = ztaps.astype(fields.dtype)
    rows = jnp.arange(3 * half_y, dtype=jnp.int32)
    row_source = 2 * (rows % half_y) + rows // half_y
    row_pick = (row_source[:, None] == jnp.arange(cap_y + 1, dtype=jnp.int32)[None, :]).astype(fields.dtype)
    row_pick = jnp.broadcast_to(row_pick, (in_chans, cap_x + 1) + row_pick.shape)
    yztaps = jnp.einsum("cxjy,cxyk->cxjk", row_pick, ztaps, preferred_element_type=jnp.float32)
    yztaps = yztaps.astype(fields.dtype)
    blocks = []
    for off_x in range(3):
        for off_y in range(3):
            blocks.append(yztaps[:, off_x : off_x + 2 * half_x - 1 : 2, off_y * half_y : (off_y + 1) * half_y])
    stacked = jnp.stack(blocks, axis=1).reshape(in_chans * 9, half_x, half_y, 3 * half_z)
    kernel = weight.reshape(out_chans, in_chans * 9, 3)
    conv = bias[:, None, None, None]
    for off_z in range(3):
        part = stacked[..., off_z * half_z : (off_z + 1) * half_z]
        conv = conv + jnp.einsum("ok,kpqr->opqr", kernel[:, :, off_z], part, preferred_element_type=jnp.float32)
    live = (row_ok[:, None] & col_ok[None, :]).reshape(1, half_x, half_y, 1)
    pre_wide = lax.reduce_precision(jnp.where(live, conv, 0.0), exponent_bits=8, mantissa_bits=7)
    sigma = jax.nn.sigmoid(pre_wide)
    stem_local = (pre_wide * sigma).astype(jnp.bfloat16)
    slope = sigma * (1.0 + pre_wide * (1.0 - sigma))
    grad_wide = jnp.where(live, cell_grad.astype(jnp.float32) * slope, 0.0)
    grad_wide = lax.reduce_precision(grad_wide, exponent_bits=8, mantissa_bits=7)
    returned = grad_wide.astype(jnp.bfloat16)
    stem = lax.all_to_all(stem_local, "gy", split_axis=0, concat_axis=2, tiled=True)
    grads = []
    for off_z in range(3):
        part = stacked[..., off_z * half_z : (off_z + 1) * half_z]
        grads.append(jnp.einsum("opqr,kpqr->ok", returned, part, preferred_element_type=jnp.float32))
    weight_full = jnp.stack(grads, axis=-1).reshape(out_chans, -1)
    bias_full = jnp.sum(grad_wide, axis=(1, 2, 3))
    packed = jnp.concatenate([weight_full, bias_full[:, None]], axis=1)
    total = butterfly_sum(butterfly_sum(packed, "gy"), "gx")
    share = out_chans // tiles_y
    mine = lax.dynamic_slice_in_dim(total, lax.axis_index("gy") * share, share, 0)
    weight_grad, bias_grad = mine[:, :-1], mine[:, -1]
    return (stem, weight_grad, bias_grad)


def solution(mesh):
    in_specs = (P(None, "gx", "gy", None), P(), P(), P(), P(), P("gy", "gx", None, None))
    out_specs = (P("gy", "gx", None, None), P("gy", None), P("gy"))
    return jax.shard_map(local, mesh=mesh, in_specs=in_specs, out_specs=out_specs, check_vma=False)
```

```python
import jax
import jax.numpy as jnp
from jax import lax
from jax.sharding import PartitionSpec as P


def from_behind(block, axis, distance):
    devices = range(lax.axis_size(axis))
    route = [(i - distance, i) for i in devices if i - distance in devices]
    return lax.ppermute(block, axis, route)


def exchange(value, axes, size, spans):
    vals = [value] + [lax.ppermute(value, axes, [(i, i ^ t) for i in range(size)]) for t in spans]
    while len(vals) > 1:
        vals = [vals[k] + vals[k + 1] for k in range(0, len(vals), 2)]
    return vals[0]


def grid_sum(value):
    nx, ny = lax.axis_size("gx"), lax.axis_size("gy")
    if nx & (nx - 1) or ny & (ny - 1):
        return lax.psum(value, ("gx", "gy"))
    bits_x, bits_y = nx.bit_length() - 1, ny.bit_length() - 1
    while bits_x >= 2:
        low = bits_x - 2
        value = exchange(value, "gx", nx, [(1 << low) * t for t in (1, 2, 3)])
        bits_x = low
    if bits_x and bits_y:
        top = 1 << (bits_y - 1)
        value = exchange(value, ("gx", "gy"), nx * ny, [top, ny, ny + top])
        bits_x, bits_y = 0, bits_y - 1
    if bits_x:
        value = exchange(value, "gx", nx, [1])
    while bits_y:
        bits_y -= 1
        value = exchange(value, "gy", ny, [1 << bits_y])
    return value


def extend(data, border, keep, at, dim):
    length = data.shape[dim]
    border_wide = jnp.expand_dims(border, dim)
    joined = jnp.concatenate([jnp.zeros_like(border_wide), data], axis=dim)
    shape = [1] * joined.ndim
    shape[dim] = length + 1
    kept = jnp.where(keep.reshape(shape), joined, jnp.zeros_like(joined))
    return jnp.where(at.reshape(shape), border_wide, kept)


def count_masks(counts, axis, length):
    here = (jnp.arange(counts.shape[0], dtype=jnp.int32) == lax.axis_index(axis))[:, None]
    places = jnp.arange(length + 1, dtype=jnp.int32)[None, :]
    edge = (length - counts)[:, None]
    keep = jnp.any(here & (places > edge), axis=0)
    at = jnp.any(here & (places == edge), axis=0)
    half = jnp.arange(length // 2, dtype=jnp.int32)[None, :]
    ok = jnp.any(here & (half >= length // 2 - (counts // 2)[:, None]), axis=0)
    return keep, at, ok


def taps(padded, axes, halves):
    pieces = []
    for off_x in range(3):
        for off_y in range(3):
            for off_z in range(3):
                piece = padded
                for axis_no, offset, half in zip(axes, (off_x, off_y, off_z), halves):
                    piece = lax.slice_in_dim(piece, offset, offset + 2 * half - 1, 2, axis_no)
                pieces.append(piece)
    return pieces


def local(fields, rows_live, cols_live, weight, bias, grad_out):
    in_chans, cap_x, cap_y, depth = fields.shape
    half_x = cap_x // 2
    half_y = cap_y // 2
    half_z = depth // 2
    out_chans = weight.shape[0]
    tiles_y = lax.axis_size("gy")
    cell_grad = lax.all_to_all(grad_out, "gy", split_axis=2, concat_axis=0, tiled=True)
    row_keep, row_at, row_ok = count_masks(rows_live, "gx", cap_x)
    col_keep, col_at, col_ok = count_masks(cols_live, "gy", cap_y)
    above = from_behind(fields[:, cap_x - 1], "gx", 1)
    ext_rows = extend(fields, above, row_keep, row_at, 1)
    beside = from_behind(ext_rows[:, :, cap_y - 1], "gy", 1)
    ext_full = extend(ext_rows, beside, col_keep, col_at, 2)
    lanes = jnp.arange(3 * half_z, dtype=jnp.int32)
    source = 2 * (lanes % half_z) + lanes // half_z - 1
    pick = (jnp.arange(depth, dtype=jnp.int32)[:, None] == source[None, :]).astype(fields.dtype)
    ztaps = jnp.einsum("cxyz,zk->cxyk", ext_full, pick, preferred_element_type=jnp.float32)
    ztaps = ztaps.astype(fields.dtype)
    rows = jnp.arange(3 * half_y, dtype=jnp.int32)
    row_source = 2 * (rows % half_y) + rows // half_y
    row_pick = (row_source[:, None] == jnp.arange(cap_y + 1, dtype=jnp.int32)[None, :]).astype(fields.dtype)
    row_pick = jnp.broadcast_to(row_pick, (in_chans, cap_x + 1) + row_pick.shape)
    yztaps = jnp.einsum("cxjy,cxyk->cxjk", row_pick, ztaps, preferred_element_type=jnp.float32)
    yztaps = yztaps.astype(fields.dtype)
    blocks = []
    for off_x in range(3):
        for off_y in range(3):
            blocks.append(yztaps[:, off_x : off_x + 2 * half_x - 1 : 2, off_y * half_y : (off_y + 1) * half_y])
    stacked = jnp.stack(blocks, axis=1).reshape(in_chans * 9, half_x, half_y, 3 * half_z)
    kernel = weight.reshape(out_chans, in_chans * 9, 3)
    conv = bias[:, None, None, None]
    for off_z in range(3):
        part = stacked[..., off_z * half_z : (off_z + 1) * half_z]
        conv = conv + jnp.einsum("ok,kpqr->opqr", kernel[:, :, off_z], part, preferred_element_type=jnp.float32)
    live = (row_ok[:, None] & col_ok[None, :]).reshape(1, half_x, half_y, 1)
    pre_wide = lax.reduce_precision(jnp.where(live, conv, 0.0), exponent_bits=8, mantissa_bits=7)
    sigma = jax.nn.sigmoid(pre_wide)
    stem_local = (pre_wide * sigma).astype(jnp.bfloat16)
    slope = sigma * (1.0 + pre_wide * (1.0 - sigma))
    grad_wide = jnp.where(live, cell_grad.astype(jnp.float32) * slope, 0.0)
    grad_wide = lax.reduce_precision(grad_wide, exponent_bits=8, mantissa_bits=7)
    returned = grad_wide.astype(jnp.bfloat16)
    stem = lax.all_to_all(stem_local, "gy", split_axis=0, concat_axis=2, tiled=True)
    grads = []
    for off_z in range(3):
        part = stacked[..., off_z * half_z : (off_z + 1) * half_z]
        grads.append(jnp.einsum("opqr,kpqr->ok", returned, part, preferred_element_type=jnp.float32))
    weight_full = jnp.stack(grads, axis=-1).reshape(out_chans, -1)
    bias_full = jnp.sum(grad_wide, axis=(1, 2, 3))
    packed = jnp.concatenate([weight_full, bias_full[:, None]], axis=1)
    total = grid_sum(packed)
    share = out_chans // tiles_y
    mine = lax.dynamic_slice_in_dim(total, lax.axis_index("gy") * share, share, 0)
    weight_grad, bias_grad = mine[:, :-1], mine[:, -1]
    return (stem, weight_grad, bias_grad)


def solution(mesh):
    in_specs = (P(None, "gx", "gy", None), P(), P(), P(), P(), P("gy", "gx", None, None))
    out_specs = (P("gy", "gx", None, None), P("gy", None), P("gy"))
    return jax.shard_map(local, mesh=mesh, in_specs=in_specs, out_specs=out_specs, check_vma=False)
```

```python
import jax
import jax.numpy as jnp
from jax import lax
from jax.sharding import PartitionSpec as P


def from_behind(block, axis, distance):
    devices = range(lax.axis_size(axis))
    route = [(i - distance, i) for i in devices if i - distance in devices]
    return lax.ppermute(block, axis, route)


def butterfly_sum(value, axis, widest=2):
    size = lax.axis_size(axis)
    if size & (size - 1):
        return lax.psum(value, axis)
    bits = size.bit_length() - 1
    while bits:
        low = max(bits - widest, 0)
        spans = [(1 << low) * t for t in range(1, 1 << (bits - low))]
        got = [lax.ppermute(value, axis, [(i, i ^ t) for i in range(size)]) for t in spans]
        if len(got) == 1:
            value = value + got[0]
        else:
            value = (value + got[0]) + (got[1] + got[2])
        bits = low
    return value


def extend(data, border, keep, at, dim):
    length = data.shape[dim]
    border_wide = jnp.expand_dims(border, dim)
    joined = jnp.concatenate([jnp.zeros_like(border_wide), data], axis=dim)
    shape = [1] * joined.ndim
    shape[dim] = length + 1
    kept = jnp.where(keep.reshape(shape), joined, jnp.zeros_like(joined))
    return jnp.where(at.reshape(shape), border_wide, kept)


def count_masks(counts, axis, length):
    here = (jnp.arange(counts.shape[0], dtype=jnp.int32) == lax.axis_index(axis))[:, None]
    places = jnp.arange(length + 1, dtype=jnp.int32)[None, :]
    edge = (length - counts)[:, None]
    keep = jnp.any(here & (places > edge), axis=0)
    at = jnp.any(here & (places == edge), axis=0)
    half = jnp.arange(length // 2, dtype=jnp.int32)[None, :]
    ok = jnp.any(here & (half >= length // 2 - (counts // 2)[:, None]), axis=0)
    return keep, at, ok


def taps(padded, axes, halves):
    pieces = []
    for off_x in range(3):
        for off_y in range(3):
            for off_z in range(3):
                piece = padded
                for axis_no, offset, half in zip(axes, (off_x, off_y, off_z), halves):
                    piece = lax.slice_in_dim(piece, offset, offset + 2 * half - 1, 2, axis_no)
                pieces.append(piece)
    return pieces


def local(fields, rows_live, cols_live, weight, bias, grad_out):
    in_chans, cap_x, cap_y, depth = fields.shape
    half_x = cap_x // 2
    half_y = cap_y // 2
    half_z = depth // 2
    out_chans = weight.shape[0]
    tiles_y = lax.axis_size("gy")
    cell_grad = lax.all_to_all(grad_out, "gy", split_axis=2, concat_axis=0, tiled=True)
    row_keep, row_at, row_ok = count_masks(rows_live, "gx", cap_x)
    col_keep, col_at, col_ok = count_masks(cols_live, "gy", cap_y)
    above = from_behind(fields[:, cap_x - 1], "gx", 1)
    ext_rows = extend(fields, above, row_keep, row_at, 1)
    beside = from_behind(ext_rows[:, :, cap_y - 1], "gy", 1)
    ext_full = extend(ext_rows, beside, col_keep, col_at, 2)
    lanes = jnp.arange(3 * half_z, dtype=jnp.int32)
    source = 2 * (lanes % half_z) + lanes // half_z - 1
    pick = (jnp.arange(depth, dtype=jnp.int32)[:, None] == source[None, :]).astype(fields.dtype)
    ztaps = jnp.einsum("cxyz,zk->cxyk", ext_full, pick, preferred_element_type=jnp.float32)
    ztaps = ztaps.astype(fields.dtype)
    rows = jnp.arange(3 * half_y, dtype=jnp.int32)
    row_source = 2 * (rows % half_y) + rows // half_y
    row_pick = (row_source[:, None] == jnp.arange(cap_y + 1, dtype=jnp.int32)[None, :]).astype(fields.dtype)
    row_pick = jnp.broadcast_to(row_pick, (in_chans, cap_x + 1) + row_pick.shape)
    yztaps = jnp.einsum("cxjy,cxyk->cxjk", row_pick, ztaps, preferred_element_type=jnp.float32)
    yztaps = yztaps.astype(fields.dtype)
    blocks = []
    for off_x in range(3):
        for off_y in range(3):
            blocks.append(yztaps[:, off_x : off_x + 2 * half_x - 1 : 2, off_y * half_y : (off_y + 1) * half_y])
    stacked = jnp.stack(blocks, axis=1).reshape(in_chans * 9, half_x, half_y, 3 * half_z)
    kernel = weight.reshape(out_chans, in_chans * 9, 3)
    conv = bias[:, None, None, None]
    for off_z in range(3):
        part = stacked[..., off_z * half_z : (off_z + 1) * half_z]
        conv = conv + jnp.einsum("ok,kpqr->opqr", kernel[:, :, off_z], part, preferred_element_type=jnp.float32)
    live = (row_ok[:, None] & col_ok[None, :]).reshape(1, half_x, half_y, 1)
    pre_wide = lax.reduce_precision(jnp.where(live, conv, 0.0), exponent_bits=8, mantissa_bits=7)
    sigma = jax.nn.sigmoid(pre_wide)
    stem_local = (pre_wide * sigma).astype(jnp.bfloat16)
    slope = sigma * (1.0 + pre_wide * (1.0 - sigma))
    grad_wide = jnp.where(live, cell_grad.astype(jnp.float32) * slope, 0.0)
    grad_wide = lax.reduce_precision(grad_wide, exponent_bits=8, mantissa_bits=7)
    returned = grad_wide.astype(jnp.bfloat16)
    stem = lax.all_to_all(stem_local, "gy", split_axis=0, concat_axis=2, tiled=True)
    grads = []
    for off_z in range(3):
        part = stacked[..., off_z * half_z : (off_z + 1) * half_z]
        grads.append(jnp.einsum("opqr,kpqr->ok", returned, part, preferred_element_type=jnp.float32))
    weight_full = jnp.stack(grads, axis=-1).reshape(out_chans, -1)
    bias_full = jnp.sum(grad_wide, axis=(1, 2, 3))
    packed = jnp.concatenate([weight_full, bias_full[:, None]], axis=1)
    total = butterfly_sum(butterfly_sum(packed, "gx"), "gy", 1)
    share = out_chans // tiles_y
    mine = lax.dynamic_slice_in_dim(total, lax.axis_index("gy") * share, share, 0)
    weight_grad, bias_grad = mine[:, :-1], mine[:, -1]
    return (stem, weight_grad, bias_grad)


def solution(mesh):
    in_specs = (P(None, "gx", "gy", None), P(), P(), P(), P(), P("gy", "gx", None, None))
    out_specs = (P("gy", "gx", None, None), P("gy", None), P("gy"))
    return jax.shard_map(local, mesh=mesh, in_specs=in_specs, out_specs=out_specs, check_vma=False)
```

```python
import jax
import jax.numpy as jnp
from jax import lax
from jax.sharding import PartitionSpec as P


def from_behind(block, axis, distance):
    devices = range(lax.axis_size(axis))
    route = [(i - distance, i) for i in devices if i - distance in devices]
    return lax.ppermute(block, axis, route)


def butterfly_sum(value, axis):
    size = lax.axis_size(axis)
    if size & (size - 1):
        return lax.psum(value, axis)
    bits = size.bit_length() - 1
    while bits:
        low = max(bits - 2, 0)
        spans = [(1 << low) * t for t in range(1, 1 << (bits - low))]
        got = [lax.ppermute(value, axis, [(i, i ^ t) for i in range(size)]) for t in spans]
        if len(got) == 1:
            value = value + got[0]
        else:
            value = (value + got[0]) + (got[1] + got[2])
        bits = low
    return value


def extend(data, border, keep, at, dim):
    length = data.shape[dim]
    border_wide = jnp.expand_dims(border, dim)
    joined = jnp.concatenate([jnp.zeros_like(border_wide), data], axis=dim)
    shape = [1] * joined.ndim
    shape[dim] = length + 1
    kept = jnp.where(keep.reshape(shape), joined, jnp.zeros_like(joined))
    return jnp.where(at.reshape(shape), border_wide, kept)


def count_masks(counts, axis, length):
    here = (jnp.arange(counts.shape[0], dtype=jnp.int32) == lax.axis_index(axis))[:, None]
    places = jnp.arange(length + 1, dtype=jnp.int32)[None, :]
    edge = (length - counts)[:, None]
    keep = jnp.any(here & (places > edge), axis=0)
    at = jnp.any(here & (places == edge), axis=0)
    half = jnp.arange(length // 2, dtype=jnp.int32)[None, :]
    ok = jnp.any(here & (half >= length // 2 - (counts // 2)[:, None]), axis=0)
    return keep, at, ok


def taps(padded, axes, halves):
    pieces = []
    for off_x in range(3):
        for off_y in range(3):
            for off_z in range(3):
                piece = padded
                for axis_no, offset, half in zip(axes, (off_x, off_y, off_z), halves):
                    piece = lax.slice_in_dim(piece, offset, offset + 2 * half - 1, 2, axis_no)
                pieces.append(piece)
    return pieces


def local(fields, rows_live, cols_live, weight, bias, grad_out):
    in_chans, cap_x, cap_y, depth = fields.shape
    half_x = cap_x // 2
    half_y = cap_y // 2
    half_z = depth // 2
    out_chans = weight.shape[0]
    tiles_y = lax.axis_size("gy")
    cell_grad = lax.all_to_all(grad_out, "gy", split_axis=2, concat_axis=0, tiled=True)
    row_keep, row_at, row_ok = count_masks(rows_live, "gx", cap_x)
    col_keep, col_at, col_ok = count_masks(cols_live, "gy", cap_y)
    above = from_behind(fields[:, cap_x - 1], "gx", 1)
    ext_rows = extend(fields, above, row_keep, row_at, 1)
    beside = from_behind(ext_rows[:, :, cap_y - 1], "gy", 1)
    ext_full = extend(ext_rows, beside, col_keep, col_at, 2)
    lanes = jnp.arange(3 * half_z, dtype=jnp.int32)
    source = 2 * (lanes % half_z) + lanes // half_z - 1
    pick = (jnp.arange(depth, dtype=jnp.int32)[:, None] == source[None, :]).astype(fields.dtype)
    ztaps = jnp.einsum("cxyz,zk->cxyk", ext_full, pick, preferred_element_type=jnp.float32)
    ztaps = ztaps.astype(fields.dtype)
    rows = jnp.arange(3 * half_y, dtype=jnp.int32)
    row_source = 2 * (rows % half_y) + rows // half_y
    row_pick = (row_source[:, None] == jnp.arange(cap_y + 1, dtype=jnp.int32)[None, :]).astype(fields.dtype)
    row_pick = jnp.broadcast_to(row_pick, (in_chans, cap_x + 1) + row_pick.shape)
    yztaps = jnp.einsum("cxjy,cxyk->cxjk", row_pick, ztaps, preferred_element_type=jnp.float32)
    yztaps = yztaps.astype(fields.dtype)
    blocks = []
    for off_x in range(3):
        for off_y in range(3):
            blocks.append(yztaps[:, off_x : off_x + 2 * half_x - 1 : 2, off_y * half_y : (off_y + 1) * half_y])
    blocks = [b.reshape(b.shape[:3] + (3, half_z)).transpose(0, 3, 1, 2, 4) for b in blocks]
    patches = jnp.stack(blocks, axis=1).reshape(in_chans * 27, half_x, half_y, half_z)
    conv = jnp.einsum("ok,kpqr->opqr", weight, patches, preferred_element_type=jnp.float32)
    conv = conv + bias[:, None, None, None]
    live = (row_ok[:, None] & col_ok[None, :]).reshape(1, half_x, half_y, 1)
    pre_wide = lax.reduce_precision(jnp.where(live, conv, 0.0), exponent_bits=8, mantissa_bits=7)
    sigma = jax.nn.sigmoid(pre_wide)
    stem_local = (pre_wide * sigma).astype(jnp.bfloat16)
    slope = sigma * (1.0 + pre_wide * (1.0 - sigma))
    grad_wide = jnp.where(live, cell_grad.astype(jnp.float32) * slope, 0.0)
    grad_wide = lax.reduce_precision(grad_wide, exponent_bits=8, mantissa_bits=7)
    returned = grad_wide.astype(jnp.bfloat16)
    stem = lax.all_to_all(stem_local, "gy", split_axis=0, concat_axis=2, tiled=True)
    weight_full = jnp.einsum("opqr,kpqr->ok", returned, patches, preferred_element_type=jnp.float32)
    bias_full = jnp.sum(grad_wide, axis=(1, 2, 3))
    packed = jnp.concatenate([weight_full, bias_full[:, None]], axis=1)
    total = butterfly_sum(butterfly_sum(packed, "gx"), "gy")
    share = out_chans // tiles_y
    mine = lax.dynamic_slice_in_dim(total, lax.axis_index("gy") * share, share, 0)
    weight_grad, bias_grad = mine[:, :-1], mine[:, -1]
    return (stem, weight_grad, bias_grad)


def solution(mesh):
    in_specs = (P(None, "gx", "gy", None), P(), P(), P(), P(), P("gy", "gx", None, None))
    out_specs = (P("gy", "gx", None, None), P("gy", None), P("gy"))
    return jax.shard_map(local, mesh=mesh, in_specs=in_specs, out_specs=out_specs, check_vma=False)
```

```python
import jax
import jax.numpy as jnp
from jax import lax
from jax.sharding import PartitionSpec as P


def from_behind(block, axis, distance):
    devices = range(lax.axis_size(axis))
    route = [(i - distance, i) for i in devices if i - distance in devices]
    return lax.ppermute(block, axis, route)


def butterfly_sum(value, axis):
    size = lax.axis_size(axis)
    if size & (size - 1):
        return lax.psum(value, axis)
    bits = size.bit_length() - 1
    while bits:
        low = max(bits - 2, 0)
        spans = [(1 << low) * t for t in range(1, 1 << (bits - low))]
        got = [lax.ppermute(value, axis, [(i, i ^ t) for i in range(size)]) for t in spans]
        if len(got) == 1:
            value = value + got[0]
        else:
            value = (value + got[0]) + (got[1] + got[2])
        bits = low
    return value


def extend(data, border, keep, at, dim):
    length = data.shape[dim]
    border_wide = jnp.expand_dims(border, dim)
    joined = jnp.concatenate([jnp.zeros_like(border_wide), data], axis=dim)
    shape = [1] * joined.ndim
    shape[dim] = length + 1
    kept = jnp.where(keep.reshape(shape), joined, jnp.zeros_like(joined))
    return jnp.where(at.reshape(shape), border_wide, kept)


def count_masks(counts, axis, length):
    here = (jnp.arange(counts.shape[0], dtype=jnp.int32) == lax.axis_index(axis))[:, None]
    places = jnp.arange(length + 1, dtype=jnp.int32)[None, :]
    edge = (length - counts)[:, None]
    keep = jnp.any(here & (places > edge), axis=0)
    at = jnp.any(here & (places == edge), axis=0)
    half = jnp.arange(length // 2, dtype=jnp.int32)[None, :]
    ok = jnp.any(here & (half >= length // 2 - (counts // 2)[:, None]), axis=0)
    return keep, at, ok


def taps(padded, axes, halves):
    pieces = []
    for off_x in range(3):
        for off_y in range(3):
            for off_z in range(3):
                piece = padded
                for axis_no, offset, half in zip(axes, (off_x, off_y, off_z), halves):
                    piece = lax.slice_in_dim(piece, offset, offset + 2 * half - 1, 2, axis_no)
                pieces.append(piece)
    return pieces


def local(fields, rows_live, cols_live, weight, bias, grad_out):
    in_chans, cap_x, cap_y, depth = fields.shape
    half_x = cap_x // 2
    half_y = cap_y // 2
    half_z = depth // 2
    out_chans = weight.shape[0]
    tiles_y = lax.axis_size("gy")
    cell_grad = lax.all_to_all(grad_out, "gy", split_axis=2, concat_axis=0, tiled=True)
    row_keep, row_at, row_ok = count_masks(rows_live, "gx", cap_x)
    col_keep, col_at, col_ok = count_masks(cols_live, "gy", cap_y)
    above = from_behind(fields[:, cap_x - 1], "gx", 1)
    ext_rows = extend(fields, above, row_keep, row_at, 1)
    beside = from_behind(ext_rows[:, :, cap_y - 1], "gy", 1)
    ext_full = extend(ext_rows, beside, col_keep, col_at, 2)
    lanes = jnp.arange(3 * half_z, dtype=jnp.int32)
    source = 2 * (lanes % half_z) + lanes // half_z - 1
    pick = (jnp.arange(depth, dtype=jnp.int32)[:, None] == source[None, :]).astype(fields.dtype)
    ztaps = jnp.einsum("cxyz,zk->cxyk", ext_full, pick, preferred_element_type=jnp.float32)
    ztaps = ztaps.astype(fields.dtype)
    rows = jnp.arange(3 * half_y, dtype=jnp.int32)
    row_source = 2 * (rows % half_y) + rows // half_y
    row_pick = (row_source[:, None] == jnp.arange(cap_y + 1, dtype=jnp.int32)[None, :]).astype(fields.dtype)
    row_pick = jnp.broadcast_to(row_pick, (in_chans, cap_x + 1) + row_pick.shape)
    yztaps = jnp.einsum("cxjy,cxyk->cxjk", row_pick, ztaps, preferred_element_type=jnp.float32)
    yztaps = yztaps.astype(fields.dtype)
    blocks = []
    for off_x in range(3):
        for off_y in range(3):
            blocks.append(yztaps[:, off_x : off_x + 2 * half_x - 1 : 2, off_y * half_y : (off_y + 1) * half_y])
    stacked = jnp.stack(blocks, axis=1).reshape(in_chans * 9, half_x, half_y, 3 * half_z)
    kernel = weight.reshape(out_chans, in_chans * 9, 3)
    conv = bias[:, None, None, None]
    for off_z in range(3):
        part = stacked[..., off_z * half_z : (off_z + 1) * half_z]
        conv = conv + jnp.einsum("ok,kpqr->opqr", kernel[:, :, off_z], part, preferred_element_type=jnp.float32)
    live = (row_ok[:, None] & col_ok[None, :]).reshape(1, half_x, half_y, 1)
    pre_wide = lax.reduce_precision(jnp.where(live, conv, 0.0), exponent_bits=8, mantissa_bits=7)
    sigma = jax.nn.sigmoid(pre_wide)
    pre_out = lax.reduce_precision(jnp.where(live, lax.optimization_barrier(conv), 0.0), exponent_bits=8, mantissa_bits=7)
    stem_local = (pre_out * jax.nn.sigmoid(pre_out)).astype(jnp.bfloat16)
    slope = sigma * (1.0 + pre_wide * (1.0 - sigma))
    grad_wide = jnp.where(live, cell_grad.astype(jnp.float32) * slope, 0.0)
    grad_wide = lax.reduce_precision(grad_wide, exponent_bits=8, mantissa_bits=7)
    returned = grad_wide.astype(jnp.bfloat16)
    stem = lax.all_to_all(stem_local, "gy", split_axis=0, concat_axis=2, tiled=True)
    grads = []
    for off_z in range(3):
        part = stacked[..., off_z * half_z : (off_z + 1) * half_z]
        grads.append(jnp.einsum("opqr,kpqr->ok", returned, part, preferred_element_type=jnp.float32))
    weight_full = jnp.stack(grads, axis=-1).reshape(out_chans, -1)
    bias_full = jnp.sum(grad_wide, axis=(1, 2, 3))
    packed = jnp.concatenate([weight_full, bias_full[:, None]], axis=1)
    total = butterfly_sum(butterfly_sum(packed, "gx"), "gy")
    share = out_chans // tiles_y
    mine = lax.dynamic_slice_in_dim(total, lax.axis_index("gy") * share, share, 0)
    weight_grad, bias_grad = mine[:, :-1], mine[:, -1]
    return (stem, weight_grad, bias_grad)


def solution(mesh):
    in_specs = (P(None, "gx", "gy", None), P(), P(), P(), P(), P("gy", "gx", None, None))
    out_specs = (P("gy", "gx", None, None), P("gy", None), P("gy"))
    return jax.shard_map(local, mesh=mesh, in_specs=in_specs, out_specs=out_specs, check_vma=False)
```

```python
import jax
import jax.numpy as jnp
from jax import lax
from jax.sharding import PartitionSpec as P


def from_behind(block, axis, distance):
    devices = range(lax.axis_size(axis))
    route = [(i - distance, i) for i in devices if i - distance in devices]
    return lax.ppermute(block, axis, route)


def butterfly_sum(value, axis):
    size = lax.axis_size(axis)
    if size & (size - 1):
        return lax.psum(value, axis)
    bits = size.bit_length() - 1
    while bits:
        low = max(bits - 2, 0)
        spans = [(1 << low) * t for t in range(1, 1 << (bits - low))]
        got = [lax.ppermute(value, axis, [(i, i ^ t) for i in range(size)]) for t in spans]
        if len(got) == 1:
            value = value + got[0]
        else:
            value = (value + got[0]) + (got[1] + got[2])
        bits = low
    return value


def extend(data, border, keep, at, dim):
    length = data.shape[dim]
    border_wide = jnp.expand_dims(border, dim)
    joined = jnp.concatenate([jnp.zeros_like(border_wide), data], axis=dim)
    shape = [1] * joined.ndim
    shape[dim] = length + 1
    kept = jnp.where(keep.reshape(shape), joined, jnp.zeros_like(joined))
    return jnp.where(at.reshape(shape), border_wide, kept)


def count_masks(counts, axis, length):
    here = (jnp.arange(counts.shape[0], dtype=jnp.int32) == lax.axis_index(axis))[:, None]
    places = jnp.arange(length + 1, dtype=jnp.int32)[None, :]
    edge = (length - counts)[:, None]
    keep = jnp.any(here & (places > edge), axis=0)
    at = jnp.any(here & (places == edge), axis=0)
    half = jnp.arange(length // 2, dtype=jnp.int32)[None, :]
    ok = jnp.any(here & (half >= length // 2 - (counts // 2)[:, None]), axis=0)
    return keep, at, ok


def taps(padded, axes, halves):
    pieces = []
    for off_x in range(3):
        for off_y in range(3):
            for off_z in range(3):
                piece = padded
                for axis_no, offset, half in zip(axes, (off_x, off_y, off_z), halves):
                    piece = lax.slice_in_dim(piece, offset, offset + 2 * half - 1, 2, axis_no)
                pieces.append(piece)
    return pieces


def local(fields, rows_live, cols_live, weight, bias, grad_out):
    in_chans, cap_x, cap_y, depth = fields.shape
    half_x = cap_x // 2
    half_y = cap_y // 2
    half_z = depth // 2
    out_chans = weight.shape[0]
    tiles_y = lax.axis_size("gy")
    cell_grad = lax.all_to_all(grad_out, "gy", split_axis=2, concat_axis=0, tiled=True)
    row_keep, row_at, row_ok = count_masks(rows_live, "gx", cap_x)
    col_keep, col_at, col_ok = count_masks(cols_live, "gy", cap_y)
    above = from_behind(fields[:, cap_x - 1], "gx", 1)
    ext_rows = extend(fields, above, row_keep, row_at, 1)
    beside = from_behind(ext_rows[:, :, cap_y - 1], "gy", 1)
    ext_full = extend(ext_rows, beside, col_keep, col_at, 2)
    lanes = jnp.arange(3 * half_z, dtype=jnp.int32)
    source = 2 * (lanes % half_z) + lanes // half_z - 1
    pick = (jnp.arange(depth, dtype=jnp.int32)[:, None] == source[None, :]).astype(fields.dtype)
    ztaps = jnp.einsum("cxyz,zk->cxyk", ext_full, pick, preferred_element_type=jnp.float32)
    ztaps = ztaps.astype(fields.dtype)
    rows = jnp.arange(3 * half_y, dtype=jnp.int32)
    row_source = 2 * (rows % half_y) + rows // half_y
    row_pick = (row_source[:, None] == jnp.arange(cap_y + 1, dtype=jnp.int32)[None, :]).astype(fields.dtype)
    row_pick = jnp.broadcast_to(row_pick, (in_chans, cap_x + 1) + row_pick.shape)
    yztaps = jnp.einsum("cxjy,cxyk->cxjk", row_pick, ztaps, preferred_element_type=jnp.float32)
    yztaps = yztaps.astype(fields.dtype)
    blocks = []
    for off_x in range(3):
        for off_y in range(3):
            blocks.append(yztaps[:, off_x : off_x + 2 * half_x - 1 : 2, off_y * half_y : (off_y + 1) * half_y])
    stacked = jnp.stack(blocks, axis=1).reshape(in_chans * 9, half_x, half_y, 3 * half_z)
    kernel = weight.reshape(out_chans, in_chans * 9, 3)
    conv = bias[:, None, None, None]
    for off_z in range(3):
        part = stacked[..., off_z * half_z : (off_z + 1) * half_z]
        conv = conv + jnp.einsum("ok,kpqr->opqr", kernel[:, :, off_z], part, preferred_element_type=jnp.float32)
    live = (row_ok[:, None] & col_ok[None, :]).reshape(1, half_x, half_y, 1)
    pre_wide = lax.reduce_precision(jnp.where(live, conv, 0.0), exponent_bits=8, mantissa_bits=7)
    sigma = jax.nn.sigmoid(pre_wide)
    stem_local = (pre_wide * sigma).astype(jnp.bfloat16)
    slope = sigma * (1.0 + pre_wide * (1.0 - sigma))
    grad_wide = jnp.where(live, cell_grad.astype(jnp.float32) * slope, 0.0)
    grad_wide = lax.reduce_precision(grad_wide, exponent_bits=8, mantissa_bits=7)
    returned = grad_wide.astype(jnp.bfloat16)
    stem = lax.all_to_all(stem_local, "gy", split_axis=0, concat_axis=2, tiled=True)
    grads = []
    for off_z in range(3):
        part = stacked[..., off_z * half_z : (off_z + 1) * half_z]
        grads.append(jnp.einsum("opqr,kpqr->ok", returned, part, preferred_element_type=jnp.float32))
    weight_full = jnp.stack(grads, axis=-1).reshape(out_chans, -1)
    bias_full = jnp.sum(grad_wide, axis=(1, 2, 3))
    share = out_chans // tiles_y
    width = weight_full.shape[1]
    bias_rows = jnp.pad(bias_full.reshape(tiles_y, 1, share), ((0, 0), (0, 0), (0, width - share)))
    packed = jnp.concatenate([weight_full.reshape(tiles_y, share, width), bias_rows], axis=1)
    total = butterfly_sum(butterfly_sum(packed, "gx"), "gy")
    mine = lax.dynamic_index_in_dim(total, lax.axis_index("gy"), 0, keepdims=False)
    weight_grad, bias_grad = mine[:share], mine[share, :share]
    return (stem, weight_grad, bias_grad)


def solution(mesh):
    in_specs = (P(None, "gx", "gy", None), P(), P(), P(), P(), P("gy", "gx", None, None))
    out_specs = (P("gy", "gx", None, None), P("gy", None), P("gy"))
    return jax.shard_map(local, mesh=mesh, in_specs=in_specs, out_specs=out_specs, check_vma=False)
```

```python
import jax
import jax.numpy as jnp
from jax import lax
from jax.sharding import PartitionSpec as P


def from_behind(block, axis, distance):
    devices = range(lax.axis_size(axis))
    route = [(i - distance, i) for i in devices if i - distance in devices]
    return lax.ppermute(block, axis, route)


def butterfly_sum(value, axis):
    size = lax.axis_size(axis)
    if size & (size - 1):
        return lax.psum(value, axis)
    bits = size.bit_length() - 1
    while bits:
        low = max(bits - 2, 0)
        spans = [(1 << low) * t for t in range(1, 1 << (bits - low))]
        got = [lax.ppermute(value, axis, [(i, i ^ t) for i in range(size)]) for t in spans]
        if len(got) == 1:
            value = value + got[0]
        else:
            value = (value + got[0]) + (got[1] + got[2])
        bits = low
    return value


def extend(data, border, keep, at, dim):
    length = data.shape[dim]
    border_wide = jnp.expand_dims(border, dim)
    joined = jnp.concatenate([jnp.zeros_like(border_wide), data], axis=dim)
    shape = [1] * joined.ndim
    shape[dim] = length + 1
    kept = jnp.where(keep.reshape(shape), joined, jnp.zeros_like(joined))
    return jnp.where(at.reshape(shape), border_wide, kept)


def count_masks(counts, axis, length):
    here = (jnp.arange(counts.shape[0], dtype=jnp.int32) == lax.axis_index(axis))[:, None]
    places = jnp.arange(length + 1, dtype=jnp.int32)[None, :]
    edge = (length - counts)[:, None]
    keep = jnp.any(here & (places > edge), axis=0)
    at = jnp.any(here & (places == edge), axis=0)
    half = jnp.arange(length // 2, dtype=jnp.int32)[None, :]
    ok = jnp.any(here & (half >= length // 2 - (counts // 2)[:, None]), axis=0)
    return keep, at, ok


def taps(padded, axes, halves):
    pieces = []
    for off_x in range(3):
        for off_y in range(3):
            for off_z in range(3):
                piece = padded
                for axis_no, offset, half in zip(axes, (off_x, off_y, off_z), halves):
                    piece = lax.slice_in_dim(piece, offset, offset + 2 * half - 1, 2, axis_no)
                pieces.append(piece)
    return pieces


def local(fields, rows_live, cols_live, weight, bias, grad_out):
    in_chans, cap_x, cap_y, depth = fields.shape
    half_x = cap_x // 2
    half_y = cap_y // 2
    half_z = depth // 2
    out_chans = weight.shape[0]
    tiles_y = lax.axis_size("gy")
    cell_grad = lax.all_to_all(grad_out, "gy", split_axis=2, concat_axis=0, tiled=True)
    row_keep, row_at, row_ok = count_masks(rows_live, "gx", cap_x)
    col_keep, col_at, col_ok = count_masks(cols_live, "gy", cap_y)
    above = from_behind(fields[:, cap_x - 1], "gx", 1)
    ext_rows = extend(fields, above, row_keep, row_at, 1)
    beside = from_behind(ext_rows[:, :, cap_y - 1], "gy", 1)
    ext_full = extend(ext_rows, beside, col_keep, col_at, 2)
    lanes = jnp.arange(3 * half_z, dtype=jnp.int32)
    source = 2 * (lanes % half_z) + lanes // half_z - 1
    pick = (jnp.arange(depth, dtype=jnp.int32)[:, None] == source[None, :]).astype(fields.dtype)
    ztaps = jnp.einsum("cxyz,zk->cxyk", ext_full, pick, preferred_element_type=jnp.float32)
    ztaps = ztaps.astype(fields.dtype)
    rows = jnp.arange(3 * half_y, dtype=jnp.int32)
    row_source = 2 * (rows % half_y) + rows // half_y
    row_pick = (row_source[:, None] == jnp.arange(cap_y + 1, dtype=jnp.int32)[None, :]).astype(fields.dtype)
    row_pick = jnp.broadcast_to(row_pick, (in_chans, cap_x + 1) + row_pick.shape)
    yztaps = jnp.einsum("cxjy,cxyk->cxjk", row_pick, ztaps, preferred_element_type=jnp.float32)
    yztaps = yztaps.astype(fields.dtype)
    blocks = []
    for off_x in range(3):
        for off_y in range(3):
            blocks.append(yztaps[:, off_x : off_x + 2 * half_x - 1 : 2, off_y * half_y : (off_y + 1) * half_y])
    stacked = jnp.stack(blocks, axis=1).reshape(in_chans * 9, half_x, half_y, 3 * half_z)
    kernel = weight.reshape(out_chans, in_chans * 9, 3)
    conv = bias[:, None, None, None]
    for off_z in range(3):
        part = stacked[..., off_z * half_z : (off_z + 1) * half_z]
        conv = conv + jnp.einsum("ok,kpqr->opqr", kernel[:, :, off_z], part, preferred_element_type=jnp.float32)
    live = (row_ok[:, None] & col_ok[None, :]).reshape(1, half_x, half_y, 1)
    pre_wide = lax.reduce_precision(jnp.where(live, conv, 0.0), exponent_bits=8, mantissa_bits=7)
    sigma = jax.nn.sigmoid(pre_wide)
    stem_local = (pre_wide * sigma).astype(jnp.bfloat16)
    slope = sigma * (1.0 + pre_wide * (1.0 - sigma))
    grad_wide = jnp.where(live, cell_grad.astype(jnp.float32) * slope, 0.0)
    grad_wide = lax.reduce_precision(grad_wide, exponent_bits=8, mantissa_bits=7)
    returned = grad_wide.astype(jnp.bfloat16)
    stem = lax.all_to_all(stem_local, "gy", split_axis=0, concat_axis=2, tiled=True)
    grads = []
    for off_z in range(3):
        part = stacked[..., off_z * half_z : (off_z + 1) * half_z]
        grads.append(jnp.einsum("opqr,kpqr->ok", returned, part, preferred_element_type=jnp.float32))
    weight_full = jnp.stack(grads, axis=-1).reshape(out_chans, -1)
    bias_full = jnp.sum(grad_wide, axis=(1, 2, 3))
    share = out_chans // tiles_y
    width = weight_full.shape[1]
    bias_rows = jnp.pad(bias_full.reshape(tiles_y, share), ((0, 0), (0, width - share)))
    packed = jnp.concatenate([weight_full, bias_rows], axis=0)
    total = butterfly_sum(butterfly_sum(packed, "gx"), "gy")
    here = lax.axis_index("gy")
    weight_grad = lax.dynamic_slice_in_dim(total, here * share, share, 0)
    bias_grad = lax.dynamic_index_in_dim(total, out_chans + here, 0, keepdims=False)[:share]
    return (stem, weight_grad, bias_grad)


def solution(mesh):
    in_specs = (P(None, "gx", "gy", None), P(), P(), P(), P(), P("gy", "gx", None, None))
    out_specs = (P("gy", "gx", None, None), P("gy", None), P("gy"))
    return jax.shard_map(local, mesh=mesh, in_specs=in_specs, out_specs=out_specs, check_vma=False)
```

```python
import jax
import jax.numpy as jnp
from jax import lax
from jax.sharding import PartitionSpec as P


def from_behind(block, axis, distance):
    devices = range(lax.axis_size(axis))
    route = [(i - distance, i) for i in devices if i - distance in devices]
    return lax.ppermute(block, axis, route)


def butterfly_sum(value, axis):
    size = lax.axis_size(axis)
    if size & (size - 1):
        return lax.psum(value, axis)
    bits = size.bit_length() - 1
    base = bits % 2
    if base:
        value = value + lax.ppermute(value, axis, [(i, i ^ 1) for i in range(size)])
    while base < bits:
        spans = [(1 << base) * t for t in range(1, 4)]
        got = [lax.ppermute(value, axis, [(i, i ^ t) for i in range(size)]) for t in spans]
        value = (value + got[0]) + (got[1] + got[2])
        base += 2
    return value


def extend(data, border, keep, at, dim):
    length = data.shape[dim]
    border_wide = jnp.expand_dims(border, dim)
    joined = jnp.concatenate([jnp.zeros_like(border_wide), data], axis=dim)
    shape = [1] * joined.ndim
    shape[dim] = length + 1
    kept = jnp.where(keep.reshape(shape), joined, jnp.zeros_like(joined))
    return jnp.where(at.reshape(shape), border_wide, kept)


def count_masks(counts, axis, length):
    here = (jnp.arange(counts.shape[0], dtype=jnp.int32) == lax.axis_index(axis))[:, None]
    places = jnp.arange(length + 1, dtype=jnp.int32)[None, :]
    edge = (length - counts)[:, None]
    keep = jnp.any(here & (places > edge), axis=0)
    at = jnp.any(here & (places == edge), axis=0)
    half = jnp.arange(length // 2, dtype=jnp.int32)[None, :]
    ok = jnp.any(here & (half >= length // 2 - (counts // 2)[:, None]), axis=0)
    return keep, at, ok


def taps(padded, axes, halves):
    pieces = []
    for off_x in range(3):
        for off_y in range(3):
            for off_z in range(3):
                piece = padded
                for axis_no, offset, half in zip(axes, (off_x, off_y, off_z), halves):
                    piece = lax.slice_in_dim(piece, offset, offset + 2 * half - 1, 2, axis_no)
                pieces.append(piece)
    return pieces


def local(fields, rows_live, cols_live, weight, bias, grad_out):
    in_chans, cap_x, cap_y, depth = fields.shape
    half_x = cap_x // 2
    half_y = cap_y // 2
    half_z = depth // 2
    out_chans = weight.shape[0]
    tiles_y = lax.axis_size("gy")
    cell_grad = lax.all_to_all(grad_out, "gy", split_axis=2, concat_axis=0, tiled=True)
    row_keep, row_at, row_ok = count_masks(rows_live, "gx", cap_x)
    col_keep, col_at, col_ok = count_masks(cols_live, "gy", cap_y)
    above = from_behind(fields[:, cap_x - 1], "gx", 1)
    ext_rows = extend(fields, above, row_keep, row_at, 1)
    beside = from_behind(ext_rows[:, :, cap_y - 1], "gy", 1)
    ext_full = extend(ext_rows, beside, col_keep, col_at, 2)
    lanes = jnp.arange(3 * half_z, dtype=jnp.int32)
    source = 2 * (lanes % half_z) + lanes // half_z - 1
    pick = (jnp.arange(depth, dtype=jnp.int32)[:, None] == source[None, :]).astype(fields.dtype)
    ztaps = jnp.einsum("cxyz,zk->cxyk", ext_full, pick, preferred_element_type=jnp.float32)
    ztaps = ztaps.astype(fields.dtype)
    rows = jnp.arange(3 * half_y, dtype=jnp.int32)
    row_source = 2 * (rows % half_y) + rows // half_y
    row_pick = (row_source[:, None] == jnp.arange(cap_y + 1, dtype=jnp.int32)[None, :]).astype(fields.dtype)
    row_pick = jnp.broadcast_to(row_pick, (in_chans, cap_x + 1) + row_pick.shape)
    yztaps = jnp.einsum("cxjy,cxyk->cxjk", row_pick, ztaps, preferred_element_type=jnp.float32)
    yztaps = yztaps.astype(fields.dtype)
    blocks = []
    for off_x in range(3):
        for off_y in range(3):
            blocks.append(yztaps[:, off_x : off_x + 2 * half_x - 1 : 2, off_y * half_y : (off_y + 1) * half_y])
    stacked = jnp.stack(blocks, axis=1).reshape(in_chans * 9, half_x, half_y, 3 * half_z)
    kernel = weight.reshape(out_chans, in_chans * 9, 3)
    conv = bias[:, None, None, None]
    for off_z in range(3):
        part = stacked[..., off_z * half_z : (off_z + 1) * half_z]
        conv = conv + jnp.einsum("ok,kpqr->opqr", kernel[:, :, off_z], part, preferred_element_type=jnp.float32)
    live = (row_ok[:, None] & col_ok[None, :]).reshape(1, half_x, half_y, 1)
    pre_wide = lax.reduce_precision(jnp.where(live, conv, 0.0), exponent_bits=8, mantissa_bits=7)
    sigma = jax.nn.sigmoid(pre_wide)
    stem_local = (pre_wide * sigma).astype(jnp.bfloat16)
    slope = sigma * (1.0 + pre_wide * (1.0 - sigma))
    grad_wide = jnp.where(live, cell_grad.astype(jnp.float32) * slope, 0.0)
    grad_wide = lax.reduce_precision(grad_wide, exponent_bits=8, mantissa_bits=7)
    returned = grad_wide.astype(jnp.bfloat16)
    stem = lax.all_to_all(stem_local, "gy", split_axis=0, concat_axis=2, tiled=True)
    grads = []
    for off_z in range(3):
        part = stacked[..., off_z * half_z : (off_z + 1) * half_z]
        grads.append(jnp.einsum("opqr,kpqr->ok", returned, part, preferred_element_type=jnp.float32))
    weight_full = jnp.stack(grads, axis=-1).reshape(out_chans, -1)
    bias_full = jnp.sum(grad_wide, axis=(1, 2, 3))
    packed = jnp.concatenate([weight_full, bias_full[:, None]], axis=1)
    total = butterfly_sum(butterfly_sum(packed, "gx"), "gy")
    share = out_chans // tiles_y
    mine = lax.dynamic_slice_in_dim(total, lax.axis_index("gy") * share, share, 0)
    weight_grad, bias_grad = mine[:, :-1], mine[:, -1]
    return (stem, weight_grad, bias_grad)


def solution(mesh):
    in_specs = (P(None, "gx", "gy", None), P(), P(), P(), P(), P("gy", "gx", None, None))
    out_specs = (P("gy", "gx", None, None), P("gy", None), P("gy"))
    return jax.shard_map(local, mesh=mesh, in_specs=in_specs, out_specs=out_specs, check_vma=False)
```
